256 devices in a mesh: row: 32 (over y, x, core), col: 8 (over z).
Axes of the slice: x: 4, y: 4, z: 8, core: 2. Of those that a mesh axis runs over, the one named last changes fastest.
Arguments:
- start_block: float32 [8192, 256], P(('col', 'row')), may hold values from -6 to 6
- tile_values: float32 [32, 8, 2, 256, 256], P('row', 'col'), may hold values from -0.0625 to 0.0625
- tile_rows: int32 [32, 8, 2], P('row', 'col'), may hold values from 0 to 0, as said below
- tile_cols: int32 [32, 8, 2], P('row', 'col'), may hold values from 0 to 3
- tile_count: int32 [32, 8], P('row', 'col'), may hold values from 1 to 2, as said below
Outputs:
- image_block: float32 [8192, 256], P('row')
- new_basis: float32 [8192, 256], P(('col', 'row'))
- factor: float32 [256, 256], replicated
The draws below stay inside these ranges and needn't reach their ends.
Inputs may be any that keep to these rules, and one draw needn't show every extreme that they name: On each device the slots name distinct positions (tile_rows, tile_cols) of its 1 x 4 grid of blocks, slots at or beyond tile_count included. `tile_count`: some devices hold exactly 2 live tiles.
All inputs are finite; a program needn't handle non-finite values.
Results may differ from the reference program's by a relative error of at most 0.0001.
Values sent between devices are 32-bit elements; how exact they have to be, the bound alone decides.
No kernel may reach another device: no remote copies, remote signals or barrier semaphores. Data moves between devices by JAX's collectives and lax.ppermute only.
A program may use at most 64 MiB of HBM per device.

```python
import jax
import jax.numpy as jnp
from jax import lax

TILE = 256
K = 256
BR = 1
NB = 32
BC = 4
ORDER = 8192
TMAX = 2
N_ROW = 32
N_COL = 8


def tile_layout(key):
    device_total = N_ROW * N_COL
    key_list = jax.random.split(jax.random.fold_in(key, 11), device_total)
    shuffled = jax.vmap(lambda single_key: jax.random.permutation(single_key, BR * BC))(key_list)
    return shuffled[:, :TMAX].reshape(N_ROW, N_COL, TMAX).astype(jnp.int32)


def draw_tile_rows(key, part):
    return (tile_layout(key) // BC).astype(jnp.int32)


def draw_tile_cols(key, part):
    return (tile_layout(key) % BC).astype(jnp.int32)


def draw_tile_count(key, part):
    device_total = N_ROW * N_COL
    upper = max(2, TMAX // 3) + 1
    base_counts = jax.random.randint(jax.random.fold_in(key, 5), (device_total,), 1, upper, dtype=jnp.int32)
    ranking = jax.random.permutation(jax.random.fold_in(key, 6), device_total)
    heavy = ranking < max(1, device_total // 16)
    counts = jnp.where(heavy, TMAX, base_counts)
    return counts.reshape(N_ROW, N_COL).astype(jnp.int32)


def level_of(rng, shape, cuts, low, largest):
    def one(axis_at, parts):
        draws = jax.random.uniform(jax.random.fold_in(jax.random.fold_in(rng, 6), axis_at), (parts,), jnp.float32, low / len(cuts), largest / len(cuts))
        return jnp.repeat(jnp.exp(draws), shape[axis_at] // parts).reshape((-1,) + (1,) * (len(shape) - axis_at - 1))

    factor_of = one(*cuts[0])
    for cut in cuts[1:]:
        factor_of = factor_of * one(*cut)
    return factor_of


def normal_values(rng, dims, spread, limit, cuts=(), kind=jnp.bfloat16):
    values = jax.random.normal(rng, dims, jnp.float32) * spread
    if len(cuts) > 0:
        values = level_of(rng, dims, cuts, -0.22, 0.18) * values
    return jnp.clip(values, min=-limit, max=limit).astype(kind)


def setup_inputs(seed: int = 0) -> dict:
    arg_keys = jax.random.split(jax.random.key(seed), 6)
    return {
        "start_block": normal_values(arg_keys[0], (ORDER, K), 1.0, 6.0, ((0, 256),), jnp.float32),
        "tile_values": normal_values(arg_keys[1], (N_ROW, N_COL, TMAX, TILE, TILE), (TILE * max(1, 4 * N_COL // BR)) ** -0.5, 0.0625, ((0, 32), (1, 8)), jnp.float32),
        "tile_rows": draw_tile_rows(jax.random.fold_in(arg_keys[5], 71), 0),
        "tile_cols": draw_tile_cols(jax.random.fold_in(arg_keys[5], 71), 0),
        "tile_count": draw_tile_count(jax.random.fold_in(arg_keys[5], 71), 0),
    }


def cholesky_lower(gram):
    size = gram.shape[0]
    index = jnp.arange(size, dtype=jnp.int32)

    def column_step(j, lower):
        known = lower * (index[None, :] < j).astype(gram.dtype)
        row_j = lax.dynamic_slice_in_dim(known, j, 1, 0)[0]
        column = lax.dynamic_slice_in_dim(gram, j, 1, 1)[:, 0] - jnp.dot(known, row_j, precision=lax.Precision.HIGHEST)
        pivot = jnp.sqrt(lax.dynamic_slice_in_dim(column, j, 1, 0)[0])
        column = jnp.where(index >= j, column / pivot, jnp.zeros_like(column))
        return lax.dynamic_update_slice_in_dim(lower, column[:, None], j, 1)
    return lax.fori_loop(0, size, column_step, jnp.zeros_like(gram))

def lower_inverse(lower):
    size = lower.shape[0]
    index = jnp.arange(size, dtype=jnp.int32)

    def row_step(i, inverse):
        row_l = lax.dynamic_slice_in_dim(lower, i, 1, 0)[0]
        known = row_l * (index < i).astype(lower.dtype)
        unit = (index == i).astype(lower.dtype)
        pivot = lax.dynamic_slice_in_dim(row_l, i, 1, 0)[0]
        new_row = (unit - jnp.dot(known, inverse, precision=lax.Precision.HIGHEST)) / pivot
        return lax.dynamic_update_slice_in_dim(inverse, new_row[None, :], i, 0)
    return lax.fori_loop(0, size, row_step, jnp.zeros_like(lower))

def reference(start_block, tile_values, tile_rows, tile_cols, tile_count):
    slot_ids = jnp.arange(TMAX, dtype=jnp.int32)
    live_mask = (slot_ids[None, None, :] < tile_count[:, :, None]).astype(jnp.float32)
    global_rows = (jnp.arange(N_ROW, dtype=jnp.int32)[:, None, None] * BR + tile_rows).astype(jnp.int32)
    global_cols = (jnp.arange(N_COL, dtype=jnp.int32)[None, :, None] * BC + tile_cols).astype(jnp.int32)
    devices_all = N_ROW * N_COL
    values_all = tile_values.reshape(devices_all, TMAX, TILE, TILE)
    rows_all = global_rows.reshape(devices_all, TMAX)
    cols_all = global_cols.reshape(devices_all, TMAX)
    masks_all = live_mask.reshape(devices_all, TMAX)
    start_blocks = start_block.reshape(NB, TILE, K)

    def forward_step(accumulated, inputs):
        values, row_ids, col_ids, masks = inputs
        products = jnp.einsum('tij,tjk->tik', values, start_blocks[col_ids], precision=lax.Precision.HIGHEST, preferred_element_type=jnp.float32)
        return (accumulated.at[row_ids].add(products * masks[:, None, None]), None)
    image_blocks, _ = lax.scan(forward_step, jnp.zeros((NB, TILE, K), jnp.float32), (values_all, rows_all, cols_all, masks_all))

    def backward_step(accumulated, inputs):
        values, row_ids, col_ids, masks = inputs
        products = jnp.einsum('tji,tjk->tik', values, image_blocks[row_ids], precision=lax.Precision.HIGHEST, preferred_element_type=jnp.float32)
        return (accumulated.at[col_ids].add(products * masks[:, None, None]), None)
    projected_blocks, _ = lax.scan(backward_step, jnp.zeros((NB, TILE, K), jnp.float32), (values_all, rows_all, cols_all, masks_all))
    image_block = image_blocks.reshape(ORDER, K)
    projected = projected_blocks.reshape(ORDER, K)
    gram_matrix = jnp.dot(projected.T, projected, precision=lax.Precision.HIGHEST, preferred_element_type=jnp.float32) / ORDER
    lower = cholesky_lower(gram_matrix)
    inverse = lower_inverse(lower)
    factor = lower.T
    new_basis = jnp.dot(projected, inverse.T, precision=lax.Precision.HIGHEST, preferred_element_type=jnp.float32)
    return (image_block, new_basis, factor)
```

```python
import jax
import jax.numpy as jnp
from jax import lax
from jax.experimental import pallas as pl
from jax.experimental.pallas import tpu as pltpu
from jax.sharding import PartitionSpec as P

BR = 1


def chol_inv_kernel(g_ref, u_ref, w_ref, a_ref):
    n = g_ref.shape[0]
    a_ref[...] = g_ref[...]
    rr = lax.broadcasted_iota(jnp.int32, (n, n), 0)
    cc = lax.broadcasted_iota(jnp.int32, (n, n), 1)
    w_ref[...] = jnp.where(rr == cc, 1.0, 0.0).astype(jnp.float32)
    lane = lax.broadcasted_iota(jnp.int32, (1, n), 1)
    sub = lax.broadcasted_iota(jnp.int32, (n, 1), 0)
    lane128 = lax.broadcasted_iota(jnp.int32, (n, 128), 1)

    def step(j, carry):
        row = a_ref[pl.ds(j, 1), :]
        ajj = jnp.sum(jnp.where(lane == j, row, 0.0), axis=1, keepdims=True)
        piv = jnp.sqrt(ajj)
        lrow = jnp.where(lane >= j, row / piv, 0.0)
        base = pl.multiple_of((j // 128) * 128, 128)
        blk = a_ref[:, pl.ds(base, 128)]
        cola = jnp.sum(jnp.where(lane128 == j - base, blk, 0.0), axis=1, keepdims=True)
        lcol = jnp.where(sub >= j, cola / piv, 0.0)
        a_ref[...] = a_ref[...] - lcol * lrow
        u_ref[pl.ds(j, 1), :] = lrow
        wrow = w_ref[pl.ds(j, 1), :] / piv
        w_ref[...] = w_ref[...] - jnp.where(sub > j, lcol, 0.0) * wrow
        w_ref[pl.ds(j, 1), :] = wrow
        return carry

    lax.fori_loop(0, n, step, 0)

def chol_inv(g):
    n = g.shape[0]
    r = lax.broadcasted_iota(jnp.int32, (n, n), 0)
    c = lax.broadcasted_iota(jnp.int32, (n, n), 1)
    g = jnp.where(r >= c, g, g.T)
    return pl.pallas_call(
        chol_inv_kernel,
        out_shape=(jax.ShapeDtypeStruct((n, n), jnp.float32), jax.ShapeDtypeStruct((n, n), jnp.float32)),
        in_specs=[pl.BlockSpec(memory_space=pltpu.VMEM)],
        out_specs=(pl.BlockSpec(memory_space=pltpu.VMEM), pl.BlockSpec(memory_space=pltpu.VMEM)),
        scratch_shapes=[pltpu.VMEM((n, n), jnp.float32)],
    )(g)


def butterfly_sum(x, axis):
    size = lax.axis_size(axis)
    step = 1
    while step < size:
        x = x + lax.ppermute(x, axis, [(i, i ^ step) for i in range(size)])
        step *= 2
    return x


def body(start_block, tile_values, tile_rows, tile_cols, tile_count):
    tile_size = tile_values.shape[-1]
    basis_width = start_block.shape[1]
    slot_total = tile_values.shape[2]
    slab = lax.all_gather(start_block, "row", axis=0, tiled=True)
    start_blocks = slab.reshape(-1, tile_size, basis_width)
    block_cols = start_blocks.shape[0]
    values = tile_values.reshape(slot_total, tile_size, tile_size)
    row_ids = tile_rows.reshape(slot_total)
    col_ids = tile_cols.reshape(slot_total)
    live_count = tile_count.reshape(())
    block_rows = BR
    live_mask = (jnp.arange(slot_total, dtype=jnp.int32) < live_count).astype(jnp.float32)
    row_onehot = (row_ids[:, None] == jnp.arange(block_rows, dtype=jnp.int32)[None, :]).astype(
        jnp.float32
    ) * live_mask[:, None]
    products = jnp.einsum(
        "tij,tjk->tik",
        values,
        start_blocks[col_ids],
        precision=lax.Precision.HIGHEST,
        preferred_element_type=jnp.float32,
    )
    partial_image = jnp.einsum(
        "tb,tik->bik",
        row_onehot,
        products,
        precision=lax.Precision.HIGHEST,
        preferred_element_type=jnp.float32,
    )
    partial_rows = partial_image.reshape(-1, basis_width)
    image_block = butterfly_sum(partial_rows, "col")
    image_blocks = image_block.reshape(block_rows, tile_size, basis_width)
    col_onehot = (col_ids[:, None] == jnp.arange(block_cols, dtype=jnp.int32)[None, :]).astype(
        jnp.float32
    ) * live_mask[:, None]
    back_products = jnp.einsum(
        "tji,tjk->tik",
        values,
        image_blocks[row_ids],
        precision=lax.Precision.HIGHEST,
        preferred_element_type=jnp.float32,
    )
    partial_projected = jnp.einsum(
        "tc,tik->cik",
        col_onehot,
        back_products,
        precision=lax.Precision.HIGHEST,
        preferred_element_type=jnp.float32,
    )
    partial_flat = partial_projected.reshape(-1, basis_width)
    projected = lax.psum_scatter(partial_flat, "row", scatter_dimension=0, tiled=True)
    share_rows = projected.shape[0]
    matrix_order = share_rows * lax.axis_size("row") * lax.axis_size("col")
    local_gram = jnp.dot(
        projected.T, projected, precision=lax.Precision.HIGHEST, preferred_element_type=jnp.float32
    )
    gram_matrix = butterfly_sum(butterfly_sum(local_gram, "row"), "col") / matrix_order
    factor, inverse = chol_inv(gram_matrix)
    new_basis = lax.dot_general(
        projected,
        inverse,
        (((1,), (1,)), ((), ())),
        precision=lax.Precision.HIGHEST,
        preferred_element_type=jnp.float32,
    )
    return (image_block, new_basis, factor)


def solution(mesh):
    placed = (
        P(("col", "row"), None),
        P("row", "col", None, None, None),
        P("row", "col", None),
        P("row", "col", None),
        P("row", "col"),
    )
    return jax.shard_map(
        body,
        mesh=mesh,
        in_specs=placed,
        out_specs=(P("row", None), P(("col", "row"), None), P()),
        check_vma=False,
    )
```

```python
import jax
import jax.numpy as jnp
from jax import lax
from jax.experimental import pallas as pl
from jax.experimental.pallas import tpu as pltpu
from jax.sharding import PartitionSpec as P

BR = 1


def chol_inv_kernel(g_ref, u_ref, w_ref, a_ref):
    n = g_ref.shape[0]
    a_ref[...] = g_ref[...]
    rr = lax.broadcasted_iota(jnp.int32, (n, n), 0)
    cc = lax.broadcasted_iota(jnp.int32, (n, n), 1)
    w_ref[...] = jnp.where(rr == cc, 1.0, 0.0).astype(jnp.float32)
    lane = lax.broadcasted_iota(jnp.int32, (1, n), 1)
    sub = lax.broadcasted_iota(jnp.int32, (n, 1), 0)
    lane128 = lax.broadcasted_iota(jnp.int32, (n, 128), 1)

    def step(j, carry):
        row = a_ref[pl.ds(j, 1), :]
        ajj = jnp.sum(jnp.where(lane == j, row, 0.0), axis=1, keepdims=True)
        piv = jnp.sqrt(ajj)
        lrow = jnp.where(lane >= j, row / piv, 0.0)
        base = pl.multiple_of((j // 128) * 128, 128)
        blk = a_ref[:, pl.ds(base, 128)]
        cola = jnp.sum(jnp.where(lane128 == j - base, blk, 0.0), axis=1, keepdims=True)
        lcol = jnp.where(sub >= j, cola / piv, 0.0)
        a_ref[...] = a_ref[...] - lcol * lrow
        u_ref[pl.ds(j, 1), :] = lrow
        wrow = w_ref[pl.ds(j, 1), :] / piv
        w_ref[...] = w_ref[...] - jnp.where(sub > j, lcol, 0.0) * wrow
        w_ref[pl.ds(j, 1), :] = wrow
        return carry

    lax.fori_loop(0, n, step, 0)

def chol_inv(g):
    n = g.shape[0]
    r = lax.broadcasted_iota(jnp.int32, (n, n), 0)
    c = lax.broadcasted_iota(jnp.int32, (n, n), 1)
    g = jnp.where(r >= c, g, g.T)
    return pl.pallas_call(
        chol_inv_kernel,
        out_shape=(jax.ShapeDtypeStruct((n, n), jnp.float32), jax.ShapeDtypeStruct((n, n), jnp.float32)),
        in_specs=[pl.BlockSpec(memory_space=pltpu.VMEM)],
        out_specs=(pl.BlockSpec(memory_space=pltpu.VMEM), pl.BlockSpec(memory_space=pltpu.VMEM)),
        scratch_shapes=[pltpu.VMEM((n, n), jnp.float32)],
    )(g)


def butterfly_sum(x, axis):
    size = lax.axis_size(axis)
    step = 1
    while step < size:
        x = x + lax.ppermute(x, axis, [(i, i ^ step) for i in range(size)])
        step *= 2
    return x


def butterfly_gather(x, axis):
    size = lax.axis_size(axis)
    me = lax.axis_index(axis)
    rows, width = x.shape
    buf = x[None]
    step = size // 2
    while step >= 1:
        other = lax.ppermute(buf, axis, [(i, i ^ step) for i in range(size)])
        upper = (me // step) % 2 == 1
        low = jnp.where(upper, other, buf)
        high = jnp.where(upper, buf, other)
        buf = jnp.stack([low, high], axis=1).reshape(-1, rows, width)
        step //= 2
    return buf.reshape(-1, width)

def butterfly_scatter(x, axis):
    size = lax.axis_size(axis)
    me = lax.axis_index(axis)
    rows = x.shape[0] // size
    width = x.shape[1]
    buf = x.reshape(size, rows, width)
    step = 1
    while step < size:
        pairs = buf.reshape(-1, 2, rows, width)
        upper = (me // step) % 2 == 1
        keep = jnp.where(upper, pairs[:, 1], pairs[:, 0])
        send = jnp.where(upper, pairs[:, 0], pairs[:, 1])
        buf = keep + lax.ppermute(send, axis, [(i, i ^ step) for i in range(size)])
        step *= 2
    return buf.reshape(rows, width)

def body(start_block, tile_values, tile_rows, tile_cols, tile_count):
    tile_size = tile_values.shape[-1]
    basis_width = start_block.shape[1]
    slot_total = tile_values.shape[2]
    slab = butterfly_gather(start_block, "row")
    start_blocks = slab.reshape(-1, tile_size, basis_width)
    block_cols = start_blocks.shape[0]
    values = tile_values.reshape(slot_total, tile_size, tile_size)
    row_ids = tile_rows.reshape(slot_total)
    col_ids = tile_cols.reshape(slot_total)
    live_count = tile_count.reshape(())
    block_rows = BR
    live_mask = (jnp.arange(slot_total, dtype=jnp.int32) < live_count).astype(jnp.float32)
    row_onehot = (row_ids[:, None] == jnp.arange(block_rows, dtype=jnp.int32)[None, :]).astype(
        jnp.float32
    ) * live_mask[:, None]
    products = jnp.einsum(
        "tij,tjk->tik",
        values,
        start_blocks[col_ids],
        precision=lax.Precision.HIGHEST,
        preferred_element_type=jnp.float32,
    )
    partial_image = jnp.einsum(
        "tb,tik->bik",
        row_onehot,
        products,
        precision=lax.Precision.HIGHEST,
        preferred_element_type=jnp.float32,
    )
    partial_rows = partial_image.reshape(-1, basis_width)
    image_block = butterfly_sum(partial_rows, "col")
    image_blocks = image_block.reshape(block_rows, tile_size, basis_width)
    col_onehot = (col_ids[:, None] == jnp.arange(block_cols, dtype=jnp.int32)[None, :]).astype(
        jnp.float32
    ) * live_mask[:, None]
    back_products = jnp.einsum(
        "tji,tjk->tik",
        values,
        image_blocks[row_ids],
        precision=lax.Precision.HIGHEST,
        preferred_element_type=jnp.float32,
    )
    partial_projected = jnp.einsum(
        "tc,tik->cik",
        col_onehot,
        back_products,
        precision=lax.Precision.HIGHEST,
        preferred_element_type=jnp.float32,
    )
    partial_flat = partial_projected.reshape(-1, basis_width)
    projected = butterfly_scatter(partial_flat, "row")
    share_rows = projected.shape[0]
    matrix_order = share_rows * lax.axis_size("row") * lax.axis_size("col")
    local_gram = jnp.dot(
        projected.T, projected, precision=lax.Precision.HIGHEST, preferred_element_type=jnp.float32
    )
    gram_matrix = butterfly_sum(butterfly_sum(local_gram, "row"), "col") / matrix_order
    factor, inverse = chol_inv(gram_matrix)
    new_basis = lax.dot_general(
        projected,
        inverse,
        (((1,), (1,)), ((), ())),
        precision=lax.Precision.HIGHEST,
        preferred_element_type=jnp.float32,
    )
    return (image_block, new_basis, factor)


def solution(mesh):
    placed = (
        P(("col", "row"), None),
        P("row", "col", None, None, None),
        P("row", "col", None),
        P("row", "col", None),
        P("row", "col"),
    )
    return jax.shard_map(
        body,
        mesh=mesh,
        in_specs=placed,
        out_specs=(P("row", None), P(("col", "row"), None), P()),
        check_vma=False,
    )
```

```python
import jax
import jax.numpy as jnp
from jax import lax
from jax.experimental import pallas as pl
from jax.experimental.pallas import tpu as pltpu
from jax.sharding import PartitionSpec as P

BR = 1


PHASE = 64

def chol_solve_kernel(g_ref, p_ref, u_ref, x_ref, a_ref):
    n = g_ref.shape[0]
    m = p_ref.shape[0]
    a_ref[...] = g_ref[...]
    u_ref[...] = jnp.zeros_like(u_ref)
    x_ref[...] = p_ref[...]
    for lo in range(0, n, PHASE):
        c0 = (lo // 128) * 128
        nr = n - lo
        nc = n - c0
        sub = lax.broadcasted_iota(jnp.int32, (nr, 1), 0) + lo
        lane = lax.broadcasted_iota(jnp.int32, (1, nc), 1) + c0
        win = lax.broadcasted_iota(jnp.int32, (nr, 128), 1)
        xwin = lax.broadcasted_iota(jnp.int32, (m, 128), 1)
        full = lax.broadcasted_iota(jnp.int32, (1, n), 1)

        def step(j, carry, lo=lo, c0=c0, sub=sub, lane=lane, win=win, xwin=xwin, full=full):
            row = a_ref[pl.ds(j, 1), :]
            ajj = jnp.sum(jnp.where(full == j, row, 0.0), axis=1, keepdims=True)
            piv = jnp.sqrt(ajj)
            lfull = jnp.where(full >= j, row / piv, 0.0)
            lrow = lfull[:, c0:]
            base = pl.multiple_of((j // 128) * 128, 128)
            blk = a_ref[lo:, pl.ds(base, 128)]
            cola = jnp.sum(jnp.where(win == j - base, blk, 0.0), axis=1, keepdims=True)
            lcol = jnp.where(sub >= j, cola / piv, 0.0)
            a_ref[lo:, c0:] = a_ref[lo:, c0:] - lcol * lrow
            u_ref[pl.ds(j, 1), :] = lfull
            xblk = x_ref[:, pl.ds(base, 128)]
            xcol = jnp.sum(jnp.where(xwin == j - base, xblk, 0.0), axis=1, keepdims=True) / piv
            rest = x_ref[:, c0:]
            x_ref[:, c0:] = jnp.where(lane == j, xcol, rest - xcol * jnp.where(lane > j, lrow, 0.0))
            return carry

        lax.fori_loop(lo, lo + PHASE, step, 0)

def chol_solve(g, p):
    n = g.shape[0]
    r = lax.broadcasted_iota(jnp.int32, (n, n), 0)
    c = lax.broadcasted_iota(jnp.int32, (n, n), 1)
    g = jnp.where(r >= c, g, g.T)
    return pl.pallas_call(
        chol_solve_kernel,
        out_shape=(jax.ShapeDtypeStruct((n, n), jnp.float32), jax.ShapeDtypeStruct(p.shape, jnp.float32)),
        in_specs=[pl.BlockSpec(memory_space=pltpu.VMEM)] * 2,
        out_specs=(pl.BlockSpec(memory_space=pltpu.VMEM), pl.BlockSpec(memory_space=pltpu.VMEM)),
        scratch_shapes=[pltpu.VMEM((n, n), jnp.float32)],
    )(g, p)


def group_size(axes):
    size = 1
    for axis in axes:
        size *= lax.axis_size(axis)
    return size


def exchange_sum(x, axes):
    size = group_size(axes)
    chunks = lax.all_to_all(x.reshape(size, -1, x.shape[-1]), axes, 0, 0, tiled=False)
    return jnp.sum(chunks, axis=0)


def exchange_gather(x, axes):
    size = group_size(axes)
    copies = jnp.broadcast_to(x[None], (size,) + x.shape)
    return lax.all_to_all(copies, axes, 0, 0, tiled=False).reshape(-1, x.shape[-1])


def body(start_block, tile_values, tile_rows, tile_cols, tile_count):
    tile_size = tile_values.shape[-1]
    basis_width = start_block.shape[1]
    slot_total = tile_values.shape[2]
    slab = exchange_gather(start_block, ("row",))
    start_blocks = slab.reshape(-1, tile_size, basis_width)
    block_cols = start_blocks.shape[0]
    values = tile_values.reshape(slot_total, tile_size, tile_size)
    row_ids = tile_rows.reshape(slot_total)
    col_ids = tile_cols.reshape(slot_total)
    live_count = tile_count.reshape(())
    block_rows = BR
    live_mask = (jnp.arange(slot_total, dtype=jnp.int32) < live_count).astype(jnp.float32)
    row_onehot = (row_ids[:, None] == jnp.arange(block_rows, dtype=jnp.int32)[None, :]).astype(
        jnp.float32
    ) * live_mask[:, None]
    products = jnp.einsum(
        "tij,tjk->tik",
        values,
        start_blocks[col_ids],
        precision=lax.Precision.HIGHEST,
        preferred_element_type=jnp.float32,
    )
    partial_image = jnp.einsum(
        "tb,tik->bik",
        row_onehot,
        products,
        precision=lax.Precision.HIGHEST,
        preferred_element_type=jnp.float32,
    )
    partial_rows = partial_image.reshape(-1, basis_width)
    image_block = exchange_gather(exchange_sum(partial_rows, ("col",)), ("col",))
    image_blocks = image_block.reshape(block_rows, tile_size, basis_width)
    col_onehot = (col_ids[:, None] == jnp.arange(block_cols, dtype=jnp.int32)[None, :]).astype(
        jnp.float32
    ) * live_mask[:, None]
    back_products = jnp.einsum(
        "tji,tjk->tik",
        values,
        image_blocks[row_ids],
        precision=lax.Precision.HIGHEST,
        preferred_element_type=jnp.float32,
    )
    partial_projected = jnp.einsum(
        "tc,tik->cik",
        col_onehot,
        back_products,
        precision=lax.Precision.HIGHEST,
        preferred_element_type=jnp.float32,
    )
    partial_flat = partial_projected.reshape(-1, basis_width)
    projected = exchange_sum(partial_flat, ("row",))
    share_rows = projected.shape[0]
    matrix_order = share_rows * lax.axis_size("row") * lax.axis_size("col")
    local_gram = jnp.dot(
        projected.T, projected, precision=lax.Precision.HIGHEST, preferred_element_type=jnp.float32
    )
    both = ("row", "col")
    gram_matrix = exchange_gather(exchange_sum(local_gram, both), both) / matrix_order
    factor, new_basis = chol_solve(gram_matrix, projected)
    return (image_block, new_basis, factor)


def solution(mesh):
    placed = (
        P(("col", "row"), None),
        P("row", "col", None, None, None),
        P("row", "col", None),
        P("row", "col", None),
        P("row", "col"),
    )
    return jax.shard_map(
        body,
        mesh=mesh,
        in_specs=placed,
        out_specs=(P("row", None), P(("col", "row"), None), P()),
        check_vma=False,
    )
```

```python
import jax
import jax.numpy as jnp
from jax import lax
from jax.experimental import pallas as pl
from jax.experimental.pallas import tpu as pltpu
from jax.sharding import PartitionSpec as P

BR = 1


PHASE = 32

def chol_solve_kernel(g_ref, p_ref, u_ref, x_ref, a_ref):
    n = g_ref.shape[0]
    m = p_ref.shape[0]
    a_ref[...] = g_ref[...]
    u_ref[...] = jnp.zeros_like(u_ref)
    x_ref[...] = p_ref[...]
    for lo in range(0, n, PHASE):
        c0 = (lo // 128) * 128
        nr = n - lo
        nc = n - c0
        sub = lax.broadcasted_iota(jnp.int32, (nr, 1), 0) + lo
        lane = lax.broadcasted_iota(jnp.int32, (1, nc), 1) + c0
        win = lax.broadcasted_iota(jnp.int32, (nr, 128), 1)
        xwin = lax.broadcasted_iota(jnp.int32, (m, 128), 1)
        full = lax.broadcasted_iota(jnp.int32, (1, n), 1)

        def step(j, carry, lo=lo, c0=c0, sub=sub, lane=lane, win=win, xwin=xwin, full=full):
            row = a_ref[pl.ds(j, 1), :]
            ajj = jnp.sum(jnp.where(full == j, row, 0.0), axis=1, keepdims=True)
            inv = lax.rsqrt(ajj)
            lfull = jnp.where(full >= j, row * inv, 0.0)
            lrow = lfull[:, c0:]
            base = pl.multiple_of((j // 128) * 128, 128)
            blk = a_ref[lo:, pl.ds(base, 128)]
            cola = jnp.sum(jnp.where(win == j - base, blk, 0.0), axis=1, keepdims=True)
            lcol = jnp.where(sub >= j, cola * inv, 0.0)
            a_ref[lo:, c0:] = a_ref[lo:, c0:] - lcol * lrow
            u_ref[pl.ds(j, 1), :] = lfull
            xblk = x_ref[:, pl.ds(base, 128)]
            xcol = jnp.sum(jnp.where(xwin == j - base, xblk, 0.0), axis=1, keepdims=True)
            xcol = xcol * inv
            rest = x_ref[:, c0:]
            x_ref[:, c0:] = jnp.where(lane == j, xcol, rest - xcol * jnp.where(lane > j, lrow, 0.0))
            return carry

        lax.fori_loop(lo, lo + PHASE, step, 0)

def chol_solve(g, p):
    n = g.shape[0]
    r = lax.broadcasted_iota(jnp.int32, (n, n), 0)
    c = lax.broadcasted_iota(jnp.int32, (n, n), 1)
    g = jnp.where(r >= c, g, g.T)
    return pl.pallas_call(
        chol_solve_kernel,
        out_shape=(jax.ShapeDtypeStruct((n, n), jnp.float32), jax.ShapeDtypeStruct(p.shape, jnp.float32)),
        in_specs=[pl.BlockSpec(memory_space=pltpu.VMEM)] * 2,
        out_specs=(pl.BlockSpec(memory_space=pltpu.VMEM), pl.BlockSpec(memory_space=pltpu.VMEM)),
        scratch_shapes=[pltpu.VMEM((n, n), jnp.float32)],
    )(g, p)


def group_size(axes):
    size = 1
    for axis in axes:
        size *= lax.axis_size(axis)
    return size


def exchange_sum(x, axes):
    size = group_size(axes)
    chunks = lax.all_to_all(x.reshape(size, -1, x.shape[-1]), axes, 0, 0, tiled=False)
    return jnp.sum(chunks, axis=0)


def exchange_gather(x, axes):
    size = group_size(axes)
    copies = jnp.broadcast_to(x[None], (size,) + x.shape)
    return lax.all_to_all(copies, axes, 0, 0, tiled=False).reshape(-1, x.shape[-1])


def body(start_block, tile_values, tile_rows, tile_cols, tile_count):
    tile_size = tile_values.shape[-1]
    basis_width = start_block.shape[1]
    slot_total = tile_values.shape[2]
    slab = exchange_gather(start_block, ("row",))
    start_blocks = slab.reshape(-1, tile_size, basis_width)
    block_cols = start_blocks.shape[0]
    values = tile_values.reshape(slot_total, tile_size, tile_size)
    row_ids = tile_rows.reshape(slot_total)
    col_ids = tile_cols.reshape(slot_total)
    live_count = tile_count.reshape(())
    block_rows = BR
    live_mask = (jnp.arange(slot_total, dtype=jnp.int32) < live_count).astype(jnp.float32)
    row_onehot = (row_ids[:, None] == jnp.arange(block_rows, dtype=jnp.int32)[None, :]).astype(
        jnp.float32
    ) * live_mask[:, None]
    products = jnp.einsum(
        "tij,tjk->tik",
        values,
        start_blocks[col_ids],
        precision=lax.Precision.HIGHEST,
        preferred_element_type=jnp.float32,
    )
    partial_image = jnp.einsum(
        "tb,tik->bik",
        row_onehot,
        products,
        precision=lax.Precision.HIGHEST,
        preferred_element_type=jnp.float32,
    )
    partial_rows = partial_image.reshape(-1, basis_width)
    image_block = exchange_gather(exchange_sum(partial_rows, ("col",)), ("col",))
    image_blocks = image_block.reshape(block_rows, tile_size, basis_width)
    col_onehot = (col_ids[:, None] == jnp.arange(block_cols, dtype=jnp.int32)[None, :]).astype(
        jnp.float32
    ) * live_mask[:, None]
    back_products = jnp.einsum(
        "tji,tjk->tik",
        values,
        image_blocks[row_ids],
        precision=lax.Precision.HIGHEST,
        preferred_element_type=jnp.float32,
    )
    partial_projected = jnp.einsum(
        "tc,tik->cik",
        col_onehot,
        back_products,
        precision=lax.Precision.HIGHEST,
        preferred_element_type=jnp.float32,
    )
    partial_flat = partial_projected.reshape(-1, basis_width)
    projected = exchange_sum(partial_flat, ("row",))
    share_rows = projected.shape[0]
    matrix_order = share_rows * lax.axis_size("row") * lax.axis_size("col")
    local_gram = jnp.dot(
        projected.T, projected, precision=lax.Precision.HIGHEST, preferred_element_type=jnp.float32
    )
    both = ("row", "col")
    gram_matrix = exchange_gather(exchange_sum(local_gram, both), both) / matrix_order
    factor, new_basis = chol_solve(gram_matrix, projected)
    return (image_block, new_basis, factor)


def solution(mesh):
    placed = (
        P(("col", "row"), None),
        P("row", "col", None, None, None),
        P("row", "col", None),
        P("row", "col", None),
        P("row", "col"),
    )
    return jax.shard_map(
        body,
        mesh=mesh,
        in_specs=placed,
        out_specs=(P("row", None), P(("col", "row"), None), P()),
        check_vma=False,
    )
```

```python
import jax
import jax.numpy as jnp
from jax import lax
from jax.experimental import pallas as pl
from jax.experimental.pallas import tpu as pltpu
from jax.sharding import PartitionSpec as P

BR = 1


PHASE = 32

def pick(vec, lanes, at):
    return jnp.sum(jnp.where(lanes == at, vec, 0.0), axis=1, keepdims=True)


def chol_solve_kernel(g_ref, p_ref, u_ref, x_ref, a_ref):
    n = g_ref.shape[0]
    m = p_ref.shape[0]
    a_ref[...] = g_ref[...]
    u_ref[...] = jnp.zeros_like(u_ref)
    x_ref[...] = p_ref[...]
    full = lax.broadcasted_iota(jnp.int32, (1, n), 1)
    xwin = lax.broadcasted_iota(jnp.int32, (m, 128), 1)
    for lo in range(0, n, PHASE):
        c0 = (lo // 128) * 128
        nr = n - lo
        sub = lax.broadcasted_iota(jnp.int32, (nr, 1), 0) + lo
        lane = lax.broadcasted_iota(jnp.int32, (1, n - c0), 1) + c0
        win = lax.broadcasted_iota(jnp.int32, (nr, 128), 1)

        def step(t, carry, lo=lo, c0=c0, sub=sub, lane=lane, win=win):
            j = 2 * t
            k = j + 1
            first = a_ref[pl.ds(j, 1), :]
            second = a_ref[pl.ds(k, 1), :]
            inv1 = lax.rsqrt(pick(first, full, j))
            l21 = pick(first, full, k) * inv1
            inv2 = lax.rsqrt(pick(second, full, k) - l21 * l21)
            row1 = jnp.where(full >= j, first * inv1, 0.0)
            row2 = jnp.where(full >= k, (second - l21 * row1) * inv2, 0.0)
            base = pl.multiple_of((j // 128) * 128, 128)
            blk = a_ref[lo:, pl.ds(base, 128)]
            col1 = jnp.where(sub >= j, pick(blk, win, j - base) * inv1, 0.0)
            col2 = jnp.where(sub >= k, (pick(blk, win, k - base) - col1 * l21) * inv2, 0.0)
            a_ref[lo:, c0:] = a_ref[lo:, c0:] - (col1 * row1[:, c0:] + col2 * row2[:, c0:])
            u_ref[pl.ds(j, 1), :] = row1
            u_ref[pl.ds(k, 1), :] = row2
            xblk = x_ref[:, pl.ds(base, 128)]
            x1 = pick(xblk, xwin, j - base) * inv1
            x2 = (pick(xblk, xwin, k - base) - x1 * l21) * inv2
            later = lane > k
            rest = x_ref[:, c0:] - (x1 * jnp.where(later, row1[:, c0:], 0.0) + x2 * jnp.where(later, row2[:, c0:], 0.0))
            x_ref[:, c0:] = jnp.where(lane == j, x1, jnp.where(lane == k, x2, rest))
            return carry

        lax.fori_loop(lo // 2, (lo + PHASE) // 2, step, 0)


def chol_solve(g, p):
    n = g.shape[0]
    r = lax.broadcasted_iota(jnp.int32, (n, n), 0)
    c = lax.broadcasted_iota(jnp.int32, (n, n), 1)
    g = jnp.where(r >= c, g, g.T)
    return pl.pallas_call(
        chol_solve_kernel,
        out_shape=(jax.ShapeDtypeStruct((n, n), jnp.float32), jax.ShapeDtypeStruct(p.shape, jnp.float32)),
        in_specs=[pl.BlockSpec(memory_space=pltpu.VMEM)] * 2,
        out_specs=(pl.BlockSpec(memory_space=pltpu.VMEM), pl.BlockSpec(memory_space=pltpu.VMEM)),
        scratch_shapes=[pltpu.VMEM((n, n), jnp.float32)],
    )(g, p)


def group_size(axes):
    size = 1
    for axis in axes:
        size *= lax.axis_size(axis)
    return size


def exchange_sum(x, axes):
    size = group_size(axes)
    chunks = lax.all_to_all(x.reshape(size, -1, x.shape[-1]), axes, 0, 0, tiled=False)
    return jnp.sum(chunks, axis=0)


def exchange_gather(x, axes):
    size = group_size(axes)
    copies = jnp.broadcast_to(x[None], (size,) + x.shape)
    return lax.all_to_all(copies, axes, 0, 0, tiled=False).reshape(-1, x.shape[-1])


def body(start_block, tile_values, tile_rows, tile_cols, tile_count):
    tile_size = tile_values.shape[-1]
    basis_width = start_block.shape[1]
    slot_total = tile_values.shape[2]
    slab = exchange_gather(start_block, ("row",))
    start_blocks = slab.reshape(-1, tile_size, basis_width)
    block_cols = start_blocks.shape[0]
    values = tile_values.reshape(slot_total, tile_size, tile_size)
    row_ids = tile_rows.reshape(slot_total)
    col_ids = tile_cols.reshape(slot_total)
    live_count = tile_count.reshape(())
    block_rows = BR
    live_mask = (jnp.arange(slot_total, dtype=jnp.int32) < live_count).astype(jnp.float32)
    row_onehot = (row_ids[:, None] == jnp.arange(block_rows, dtype=jnp.int32)[None, :]).astype(
        jnp.float32
    ) * live_mask[:, None]
    products = jnp.einsum(
        "tij,tjk->tik",
        values,
        start_blocks[col_ids],
        precision=lax.Precision.HIGHEST,
        preferred_element_type=jnp.float32,
    )
    partial_image = jnp.einsum(
        "tb,tik->bik",
        row_onehot,
        products,
        precision=lax.Precision.HIGHEST,
        preferred_element_type=jnp.float32,
    )
    partial_rows = partial_image.reshape(-1, basis_width)
    image_block = exchange_gather(exchange_sum(partial_rows, ("col",)), ("col",))
    image_blocks = image_block.reshape(block_rows, tile_size, basis_width)
    col_onehot = (col_ids[:, None] == jnp.arange(block_cols, dtype=jnp.int32)[None, :]).astype(
        jnp.float32
    ) * live_mask[:, None]
    back_products = jnp.einsum(
        "tji,tjk->tik",
        values,
        image_blocks[row_ids],
        precision=lax.Precision.HIGHEST,
        preferred_element_type=jnp.float32,
    )
    partial_projected = jnp.einsum(
        "tc,tik->cik",
        col_onehot,
        back_products,
        precision=lax.Precision.HIGHEST,
        preferred_element_type=jnp.float32,
    )
    partial_flat = partial_projected.reshape(-1, basis_width)
    projected = exchange_sum(partial_flat, ("row",))
    share_rows = projected.shape[0]
    matrix_order = share_rows * lax.axis_size("row") * lax.axis_size("col")
    local_gram = jnp.dot(
        projected.T, projected, precision=lax.Precision.HIGHEST, preferred_element_type=jnp.float32
    )
    both = ("row", "col")
    gram_matrix = exchange_gather(exchange_sum(local_gram, both), both) / matrix_order
    factor, new_basis = chol_solve(gram_matrix, projected)
    return (image_block, new_basis, factor)


def solution(mesh):
    placed = (
        P(("col", "row"), None),
        P("row", "col", None, None, None),
        P("row", "col", None),
        P("row", "col", None),
        P("row", "col"),
    )
    return jax.shard_map(
        body,
        mesh=mesh,
        in_specs=placed,
        out_specs=(P("row", None), P(("col", "row"), None), P()),
        check_vma=False,
    )
```

```python
import jax
import jax.numpy as jnp
from jax import lax
from jax.experimental import pallas as pl
from jax.experimental.pallas import tpu as pltpu
from jax.sharding import PartitionSpec as P

BR = 1


PHASE = 32
BLOCK = 4


def pick(vec, lanes, at):
    return jnp.sum(jnp.where(lanes == at, vec, 0.0), axis=1, keepdims=True)


def chol_solve_kernel(g_ref, p_ref, u_ref, x_ref, a_ref):
    n = g_ref.shape[0]
    m = p_ref.shape[0]
    width = BLOCK
    a_ref[...] = g_ref[...]
    u_ref[...] = jnp.zeros_like(u_ref)
    x_ref[...] = p_ref[...]
    full = lax.broadcasted_iota(jnp.int32, (1, n), 1)
    xwin = lax.broadcasted_iota(jnp.int32, (m, 128), 1)
    for lo in range(0, n, PHASE):
        c0 = (lo // 128) * 128
        nr = n - lo
        sub = lax.broadcasted_iota(jnp.int32, (nr, 1), 0) + lo
        lane = lax.broadcasted_iota(jnp.int32, (1, n - c0), 1) + c0
        win = lax.broadcasted_iota(jnp.int32, (nr, 128), 1)

        def step(t, carry, lo=lo, c0=c0, sub=sub, lane=lane, win=win):
            j0 = width * t
            base = pl.multiple_of((j0 // 128) * 128, 128)
            blk = a_ref[lo:, pl.ds(base, 128)]
            xblk = x_ref[:, pl.ds(base, 128)]
            raw = [a_ref[pl.ds(j0 + i, 1), :] for i in range(width)]
            entry = {(i, k): pick(raw[i], full, j0 + k) for i in range(width) for k in range(i, width)}
            low, inv = {}, []
            for i in range(width):
                d = entry[(i, i)]
                for q in range(i):
                    d = d - low[(i, q)] * low[(i, q)]
                inv.append(lax.rsqrt(d))
                for k in range(i + 1, width):
                    v = entry[(i, k)]
                    for q in range(i):
                        v = v - low[(k, q)] * low[(i, q)]
                    low[(k, i)] = v * inv[i]
            rows, cols, xs = [], [], []
            for i in range(width):
                j = j0 + i
                row = raw[i]
                col = pick(blk, win, j - base)
                xv = pick(xblk, xwin, j - base)
                for q in range(i):
                    row = row - low[(i, q)] * rows[q]
                    col = col - cols[q] * low[(i, q)]
                    xv = xv - xs[q] * low[(i, q)]
                rows.append(jnp.where(full >= j, row * inv[i], 0.0))
                cols.append(jnp.where(sub >= j, col * inv[i], 0.0))
                xs.append(xv * inv[i])
            update = cols[0] * rows[0][:, c0:]
            for i in range(1, width):
                update = update + cols[i] * rows[i][:, c0:]
            a_ref[lo:, c0:] = a_ref[lo:, c0:] - update
            for i in range(width):
                u_ref[pl.ds(j0 + i, 1), :] = rows[i]
            later = lane >= j0 + width
            rest = x_ref[:, c0:]
            for i in range(width):
                rest = rest - xs[i] * jnp.where(later, rows[i][:, c0:], 0.0)
            for i in range(width):
                rest = jnp.where(lane == j0 + i, xs[i], rest)
            x_ref[:, c0:] = rest
            return carry

        lax.fori_loop(lo // width, (lo + PHASE) // width, step, 0)


def chol_solve(g, p):
    n = g.shape[0]
    r = lax.broadcasted_iota(jnp.int32, (n, n), 0)
    c = lax.broadcasted_iota(jnp.int32, (n, n), 1)
    g = jnp.where(r >= c, g, g.T)
    return pl.pallas_call(
        chol_solve_kernel,
        out_shape=(jax.ShapeDtypeStruct((n, n), jnp.float32), jax.ShapeDtypeStruct(p.shape, jnp.float32)),
        in_specs=[pl.BlockSpec(memory_space=pltpu.VMEM)] * 2,
        out_specs=(pl.BlockSpec(memory_space=pltpu.VMEM), pl.BlockSpec(memory_space=pltpu.VMEM)),
        scratch_shapes=[pltpu.VMEM((n, n), jnp.float32)],
    )(g, p)


def group_size(axes):
    size = 1
    for axis in axes:
        size *= lax.axis_size(axis)
    return size


def exchange_sum(x, axes):
    size = group_size(axes)
    chunks = lax.all_to_all(x.reshape(size, -1, x.shape[-1]), axes, 0, 0, tiled=False)
    return jnp.sum(chunks, axis=0)


def exchange_gather(x, axes):
    size = group_size(axes)
    copies = jnp.broadcast_to(x[None], (size,) + x.shape)
    return lax.all_to_all(copies, axes, 0, 0, tiled=False).reshape(-1, x.shape[-1])


def body(start_block, tile_values, tile_rows, tile_cols, tile_count):
    tile_size = tile_values.shape[-1]
    basis_width = start_block.shape[1]
    slot_total = tile_values.shape[2]
    slab = exchange_gather(start_block, ("row",))
    start_blocks = slab.reshape(-1, tile_size, basis_width)
    block_cols = start_blocks.shape[0]
    values = tile_values.reshape(slot_total, tile_size, tile_size)
    row_ids = tile_rows.reshape(slot_total)
    col_ids = tile_cols.reshape(slot_total)
    live_count = tile_count.reshape(())
    block_rows = BR
    live_mask = (jnp.arange(slot_total, dtype=jnp.int32) < live_count).astype(jnp.float32)
    row_onehot = (row_ids[:, None] == jnp.arange(block_rows, dtype=jnp.int32)[None, :]).astype(
        jnp.float32
    ) * live_mask[:, None]
    products = jnp.einsum(
        "tij,tjk->tik",
        values,
        start_blocks[col_ids],
        precision=lax.Precision.HIGHEST,
        preferred_element_type=jnp.float32,
    )
    partial_image = jnp.einsum(
        "tb,tik->bik",
        row_onehot,
        products,
        precision=lax.Precision.HIGHEST,
        preferred_element_type=jnp.float32,
    )
    partial_rows = partial_image.reshape(-1, basis_width)
    image_block = exchange_gather(exchange_sum(partial_rows, ("col",)), ("col",))
    image_blocks = image_block.reshape(block_rows, tile_size, basis_width)
    col_onehot = (col_ids[:, None] == jnp.arange(block_cols, dtype=jnp.int32)[None, :]).astype(
        jnp.float32
    ) * live_mask[:, None]
    back_products = jnp.einsum(
        "tji,tjk->tik",
        values,
        image_blocks[row_ids],
        precision=lax.Precision.HIGHEST,
        preferred_element_type=jnp.float32,
    )
    partial_projected = jnp.einsum(
        "tc,tik->cik",
        col_onehot,
        back_products,
        precision=lax.Precision.HIGHEST,
        preferred_element_type=jnp.float32,
    )
    partial_flat = partial_projected.reshape(-1, basis_width)
    projected = exchange_sum(partial_flat, ("row",))
    share_rows = projected.shape[0]
    matrix_order = share_rows * lax.axis_size("row") * lax.axis_size("col")
    local_gram = jnp.dot(
        projected.T, projected, precision=lax.Precision.HIGHEST, preferred_element_type=jnp.float32
    )
    both = ("row", "col")
    gram_matrix = exchange_gather(exchange_sum(local_gram, both), both) / matrix_order
    factor, new_basis = chol_solve(gram_matrix, projected)
    return (image_block, new_basis, factor)


def solution(mesh):
    placed = (
        P(("col", "row"), None),
        P("row", "col", None, None, None),
        P("row", "col", None),
        P("row", "col", None),
        P("row", "col"),
    )
    return jax.shard_map(
        body,
        mesh=mesh,
        in_specs=placed,
        out_specs=(P("row", None), P(("col", "row"), None), P()),
        check_vma=False,
    )
```

```python
import jax
import jax.numpy as jnp
from jax import lax
from jax.experimental import pallas as pl
from jax.experimental.pallas import tpu as pltpu
from jax.sharding import PartitionSpec as P

BR = 1


PHASE = 32
BLOCK = 4


def pick(vec, lanes, at):
    return jnp.sum(jnp.where(lanes == at, vec, 0.0), axis=1, keepdims=True)


def chol_solve_kernel(g_ref, p_ref, u_ref, x_ref, a_ref):
    n = g_ref.shape[0]
    m = p_ref.shape[0]
    width = BLOCK
    a_ref[...] = g_ref[...]
    u_ref[...] = jnp.zeros_like(u_ref)
    x_ref[...] = p_ref[...]
    full = lax.broadcasted_iota(jnp.int32, (1, n), 1)
    xwin = lax.broadcasted_iota(jnp.int32, (m, 128), 1)
    for lo in range(0, n, PHASE):
        c0 = (lo // 128) * 128
        nr = n - lo
        sub = lax.broadcasted_iota(jnp.int32, (nr, 1), 0) + lo
        lane = lax.broadcasted_iota(jnp.int32, (1, n - c0), 1) + c0
        win = lax.broadcasted_iota(jnp.int32, (nr, 128), 1)

        def step(t, carry, lo=lo, c0=c0, sub=sub, lane=lane, win=win):
            j0 = width * t
            base = pl.multiple_of((j0 // 128) * 128, 128)
            blk = a_ref[lo:, pl.ds(base, 128)]
            xblk = x_ref[:, pl.ds(base, 128)]
            raw = [a_ref[pl.ds(j0 + i, 1), :] for i in range(width)]
            entry = {(i, k): pick(raw[i], full, j0 + k) for i in range(width) for k in range(i, width)}
            low, inv = {}, []
            for i in range(width):
                d = entry[(i, i)]
                for q in range(i):
                    d = d - low[(i, q)] * low[(i, q)]
                inv.append(lax.rsqrt(d))
                for k in range(i + 1, width):
                    v = entry[(i, k)]
                    for q in range(i):
                        v = v - low[(k, q)] * low[(i, q)]
                    low[(k, i)] = v * inv[i]
            rows, cols, xs = [], [], []
            for i in range(width):
                j = j0 + i
                row = raw[i]
                col = pick(blk, win, j - base)
                xv = pick(xblk, xwin, j - base)
                for q in range(i):
                    row = row - low[(i, q)] * rows[q]
                    col = col - cols[q] * low[(i, q)]
                    xv = xv - xs[q] * low[(i, q)]
                rows.append(jnp.where(full >= j, row * inv[i], 0.0))
                cols.append(jnp.where(sub >= j, col * inv[i], 0.0))
                xs.append(xv * inv[i])
            update = cols[0] * rows[0][:, c0:]
            for i in range(1, width):
                update = update + cols[i] * rows[i][:, c0:]
            a_ref[lo:, c0:] = a_ref[lo:, c0:] - update
            for i in range(width):
                u_ref[pl.ds(j0 + i, 1), :] = rows[i]
            later = lane >= j0 + width
            rest = x_ref[:, c0:]
            for i in range(width):
                rest = rest - xs[i] * jnp.where(later, rows[i][:, c0:], 0.0)
            for i in range(width):
                rest = jnp.where(lane == j0 + i, xs[i], rest)
            x_ref[:, c0:] = rest
            return carry

        lax.fori_loop(lo // width, (lo + PHASE) // width, step, 0)


def chol_solve(g, p):
    n = g.shape[0]
    r = lax.broadcasted_iota(jnp.int32, (n, n), 0)
    c = lax.broadcasted_iota(jnp.int32, (n, n), 1)
    g = jnp.where(r >= c, g, g.T)
    return pl.pallas_call(
        chol_solve_kernel,
        out_shape=(jax.ShapeDtypeStruct((n, n), jnp.float32), jax.ShapeDtypeStruct(p.shape, jnp.float32)),
        in_specs=[pl.BlockSpec(memory_space=pltpu.VMEM)] * 2,
        out_specs=(pl.BlockSpec(memory_space=pltpu.VMEM), pl.BlockSpec(memory_space=pltpu.VMEM)),
        scratch_shapes=[pltpu.VMEM((n, n), jnp.float32)],
    )(g, p)


def group_size(axes):
    size = 1
    for axis in axes:
        size *= lax.axis_size(axis)
    return size


def exchange_sum(x, axes):
    size = group_size(axes)
    chunks = lax.all_to_all(x.reshape(size, -1, x.shape[-1]), axes, 0, 0, tiled=False)
    return jnp.sum(chunks, axis=0)


def exchange_gather(x, axes):
    size = group_size(axes)
    copies = jnp.broadcast_to(x[None], (size,) + x.shape)
    return lax.all_to_all(copies, axes, 0, 0, tiled=False).reshape(-1, x.shape[-1])


def pair_gather(x):
    other = lax.ppermute(x, "core", [(0, 1), (1, 0)])
    first = lax.axis_index("core") == 0
    return jnp.concatenate([jnp.where(first, x, other), jnp.where(first, other, x)], axis=0)


def pair_scatter_sum(x):
    chips = lax.axis_size("chip")
    pairs = x.reshape(chips, 2, -1, x.shape[-1])
    first = lax.axis_index("core") == 0
    keep = jnp.where(first, pairs[:, 0], pairs[:, 1])
    send = jnp.where(first, pairs[:, 1], pairs[:, 0])
    return (keep + lax.ppermute(send, "core", [(0, 1), (1, 0)])).reshape(-1, x.shape[-1])


def body(start_block, tile_values, tile_rows, tile_cols, tile_count):
    tile_size = tile_values.shape[-1]
    basis_width = start_block.shape[1]
    slot_total = tile_values.shape[2]
    slab = exchange_gather(pair_gather(start_block), ("chip",))
    start_blocks = slab.reshape(-1, tile_size, basis_width)
    block_cols = start_blocks.shape[0]
    values = tile_values.reshape(slot_total, tile_size, tile_size)
    row_ids = tile_rows.reshape(slot_total)
    col_ids = tile_cols.reshape(slot_total)
    live_count = tile_count.reshape(())
    block_rows = BR
    live_mask = (jnp.arange(slot_total, dtype=jnp.int32) < live_count).astype(jnp.float32)
    row_onehot = (row_ids[:, None] == jnp.arange(block_rows, dtype=jnp.int32)[None, :]).astype(
        jnp.float32
    ) * live_mask[:, None]
    products = jnp.einsum(
        "tij,tjk->tik",
        values,
        start_blocks[col_ids],
        precision=lax.Precision.HIGHEST,
        preferred_element_type=jnp.float32,
    )
    partial_image = jnp.einsum(
        "tb,tik->bik",
        row_onehot,
        products,
        precision=lax.Precision.HIGHEST,
        preferred_element_type=jnp.float32,
    )
    partial_rows = partial_image.reshape(-1, basis_width)
    image_block = exchange_gather(exchange_sum(partial_rows, ("col",)), ("col",))
    image_blocks = image_block.reshape(block_rows, tile_size, basis_width)
    col_onehot = (col_ids[:, None] == jnp.arange(block_cols, dtype=jnp.int32)[None, :]).astype(
        jnp.float32
    ) * live_mask[:, None]
    back_products = jnp.einsum(
        "tji,tjk->tik",
        values,
        image_blocks[row_ids],
        precision=lax.Precision.HIGHEST,
        preferred_element_type=jnp.float32,
    )
    partial_projected = jnp.einsum(
        "tc,tik->cik",
        col_onehot,
        back_products,
        precision=lax.Precision.HIGHEST,
        preferred_element_type=jnp.float32,
    )
    partial_flat = partial_projected.reshape(-1, basis_width)
    projected = exchange_sum(pair_scatter_sum(partial_flat), ("chip",))
    share_rows = projected.shape[0]
    matrix_order = share_rows * group_size(("chip", "core", "col"))
    local_gram = jnp.dot(
        projected.T, projected, precision=lax.Precision.HIGHEST, preferred_element_type=jnp.float32
    )
    both = ("chip", "core", "col")
    gram_matrix = exchange_gather(exchange_sum(local_gram, both), both) / matrix_order
    factor, new_basis = chol_solve(gram_matrix, projected)
    return (image_block, new_basis, factor)


def solution(mesh):
    devices = mesh.devices
    split = jax.sharding.Mesh(
        devices.reshape(devices.shape[0] // 2, 2, devices.shape[1]), ("chip", "core", "col")
    )
    rows = ("chip", "core")
    placed = (
        P(("col",) + rows, None),
        P(rows, "col", None, None, None),
        P(rows, "col", None),
        P(rows, "col", None),
        P(rows, "col"),
    )
    return jax.shard_map(
        body,
        mesh=split,
        in_specs=placed,
        out_specs=(P(rows, None), P(("col",) + rows, None), P()),
        check_vma=False,
    )
```

```python
import jax
import jax.numpy as jnp
from jax import lax
from jax.experimental import pallas as pl
from jax.experimental.pallas import tpu as pltpu
from jax.sharding import PartitionSpec as P

BR = 1


PHASE = 32
BLOCK = 4


def pick(vec, lanes, at):
    return jnp.sum(jnp.where(lanes == at, vec, 0.0), axis=1, keepdims=True)


def chol_solve_kernel(g_ref, p_ref, u_ref, x_ref, a_ref):
    n = g_ref.shape[0]
    m = p_ref.shape[0]
    width = BLOCK
    a_ref[...] = g_ref[...]
    u_ref[...] = jnp.zeros_like(u_ref)
    x_ref[...] = p_ref[...]
    full = lax.broadcasted_iota(jnp.int32, (1, n), 1)
    xwin = lax.broadcasted_iota(jnp.int32, (m, 128), 1)
    for lo in range(0, n, PHASE):
        c0 = (lo // 128) * 128
        nr = n - lo
        sub = lax.broadcasted_iota(jnp.int32, (nr, 1), 0) + lo
        lane = lax.broadcasted_iota(jnp.int32, (1, n - c0), 1) + c0
        win = lax.broadcasted_iota(jnp.int32, (nr, 128), 1)

        def step(t, carry, lo=lo, c0=c0, sub=sub, lane=lane, win=win):
            j0 = width * t
            base = pl.multiple_of((j0 // 128) * 128, 128)
            blk = a_ref[lo:, pl.ds(base, 128)]
            xblk = x_ref[:, pl.ds(base, 128)]
            raw = [a_ref[pl.ds(j0 + i, 1), :] for i in range(width)]
            entry = {(i, k): pick(raw[i], full, j0 + k) for i in range(width) for k in range(i, width)}
            low, inv = {}, []
            for i in range(width):
                d = entry[(i, i)]
                for q in range(i):
                    d = d - low[(i, q)] * low[(i, q)]
                inv.append(lax.rsqrt(d))
                for k in range(i + 1, width):
                    v = entry[(i, k)]
                    for q in range(i):
                        v = v - low[(k, q)] * low[(i, q)]
                    low[(k, i)] = v * inv[i]
            rows, cols, xs = [], [], []
            for i in range(width):
                j = j0 + i
                row = raw[i]
                col = pick(blk, win, j - base)
                xv = pick(xblk, xwin, j - base)
                for q in range(i):
                    row = row - low[(i, q)] * rows[q]
                    col = col - cols[q] * low[(i, q)]
                    xv = xv - xs[q] * low[(i, q)]
                rows.append(jnp.where(full >= j, row * inv[i], 0.0))
                cols.append(jnp.where(sub >= j, col * inv[i], 0.0))
                xs.append(xv * inv[i])
            update = cols[0] * rows[0][:, c0:]
            for i in range(1, width):
                update = update + cols[i] * rows[i][:, c0:]
            a_ref[lo:, c0:] = a_ref[lo:, c0:] - update
            for i in range(width):
                u_ref[pl.ds(j0 + i, 1), :] = rows[i]
            later = lane >= j0 + width
            rest = x_ref[:, c0:]
            for i in range(width):
                rest = rest - xs[i] * jnp.where(later, rows[i][:, c0:], 0.0)
            for i in range(width):
                rest = jnp.where(lane == j0 + i, xs[i], rest)
            x_ref[:, c0:] = rest
            return carry

        lax.fori_loop(lo // width, (lo + PHASE) // width, step, 0)


def chol_solve(g, p):
    n = g.shape[0]
    r = lax.broadcasted_iota(jnp.int32, (n, n), 0)
    c = lax.broadcasted_iota(jnp.int32, (n, n), 1)
    g = jnp.where(r >= c, g, g.T)
    return pl.pallas_call(
        chol_solve_kernel,
        out_shape=(jax.ShapeDtypeStruct((n, n), jnp.float32), jax.ShapeDtypeStruct(p.shape, jnp.float32)),
        in_specs=[pl.BlockSpec(memory_space=pltpu.VMEM)] * 2,
        out_specs=(pl.BlockSpec(memory_space=pltpu.VMEM), pl.BlockSpec(memory_space=pltpu.VMEM)),
        scratch_shapes=[pltpu.VMEM((n, n), jnp.float32)],
    )(g, p)


def group_size(axes):
    size = 1
    for axis in axes:
        size *= lax.axis_size(axis)
    return size


def exchange_sum(x, axes):
    size = group_size(axes)
    chunks = lax.all_to_all(x.reshape(size, -1, x.shape[-1]), axes, 0, 0, tiled=False)
    return jnp.sum(chunks, axis=0)


def exchange_gather(x, axes):
    size = group_size(axes)
    copies = jnp.broadcast_to(x[None], (size,) + x.shape)
    return lax.all_to_all(copies, axes, 0, 0, tiled=False).reshape(-1, x.shape[-1])


def pair_gather(x):
    other = lax.ppermute(x, "core", [(0, 1), (1, 0)])
    first = lax.axis_index("core") == 0
    low = jnp.where(first, x, other).reshape(lax.axis_size("chip"), -1, x.shape[-1])
    high = jnp.where(first, other, x).reshape(lax.axis_size("chip"), -1, x.shape[-1])
    return jnp.stack([low, high], axis=1).reshape(-1, x.shape[-1])


def pair_scatter_sum(x):
    chips = lax.axis_size("chip")
    pairs = x.reshape(chips, 2, -1, x.shape[-1])
    first = lax.axis_index("core") == 0
    keep = jnp.where(first, pairs[:, 0], pairs[:, 1])
    send = jnp.where(first, pairs[:, 1], pairs[:, 0])
    return (keep + lax.ppermute(send, "core", [(0, 1), (1, 0)])).reshape(-1, x.shape[-1])


def body(start_block, tile_values, tile_rows, tile_cols, tile_count):
    tile_size = tile_values.shape[-1]
    basis_width = start_block.shape[1]
    slot_total = tile_values.shape[2]
    slab = pair_gather(exchange_gather(start_block, ("chip",)))
    start_blocks = slab.reshape(-1, tile_size, basis_width)
    block_cols = start_blocks.shape[0]
    values = tile_values.reshape(slot_total, tile_size, tile_size)
    row_ids = tile_rows.reshape(slot_total)
    col_ids = tile_cols.reshape(slot_total)
    live_count = tile_count.reshape(())
    block_rows = BR
    live_mask = (jnp.arange(slot_total, dtype=jnp.int32) < live_count).astype(jnp.float32)
    row_onehot = (row_ids[:, None] == jnp.arange(block_rows, dtype=jnp.int32)[None, :]).astype(
        jnp.float32
    ) * live_mask[:, None]
    products = jnp.einsum(
        "tij,tjk->tik",
        values,
        start_blocks[col_ids],
        precision=lax.Precision.HIGHEST,
        preferred_element_type=jnp.float32,
    )
    partial_image = jnp.einsum(
        "tb,tik->bik",
        row_onehot,
        products,
        precision=lax.Precision.HIGHEST,
        preferred_element_type=jnp.float32,
    )
    partial_rows = partial_image.reshape(-1, basis_width)
    image_block = exchange_gather(exchange_sum(partial_rows, ("col",)), ("col",))
    image_blocks = image_block.reshape(block_rows, tile_size, basis_width)
    col_onehot = (col_ids[:, None] == jnp.arange(block_cols, dtype=jnp.int32)[None, :]).astype(
        jnp.float32
    ) * live_mask[:, None]
    back_products = jnp.einsum(
        "tji,tjk->tik",
        values,
        image_blocks[row_ids],
        precision=lax.Precision.HIGHEST,
        preferred_element_type=jnp.float32,
    )
    partial_projected = jnp.einsum(
        "tc,tik->cik",
        col_onehot,
        back_products,
        precision=lax.Precision.HIGHEST,
        preferred_element_type=jnp.float32,
    )
    partial_flat = partial_projected.reshape(-1, basis_width)
    projected = exchange_sum(pair_scatter_sum(partial_flat), ("chip",))
    share_rows = projected.shape[0]
    matrix_order = share_rows * group_size(("chip", "core", "col"))
    local_gram = jnp.dot(
        projected.T, projected, precision=lax.Precision.HIGHEST, preferred_element_type=jnp.float32
    )
    spread = ("chip", "col")
    gram_rows = exchange_gather(exchange_sum(pair_scatter_sum(local_gram), spread), spread)
    gram_matrix = pair_gather(gram_rows) / matrix_order
    factor, new_basis = chol_solve(gram_matrix, projected)
    return (image_block, new_basis, factor)


def solution(mesh):
    devices = mesh.devices
    split = jax.sharding.Mesh(
        devices.reshape(devices.shape[0] // 2, 2, devices.shape[1]), ("chip", "core", "col")
    )
    rows = ("chip", "core")
    placed = (
        P(("col",) + rows, None),
        P(rows, "col", None, None, None),
        P(rows, "col", None),
        P(rows, "col", None),
        P(rows, "col"),
    )
    return jax.shard_map(
        body,
        mesh=split,
        in_specs=placed,
        out_specs=(P(rows, None), P(("col",) + rows, None), P()),
        check_vma=False,
    )
```

```python
import jax
import jax.numpy as jnp
from jax import lax
from jax.experimental import pallas as pl
from jax.experimental.pallas import tpu as pltpu
from jax.sharding import PartitionSpec as P

BR = 1


PHASE = 32
BLOCK = 4


def pick(vec, lanes, at):
    return jnp.sum(jnp.where(lanes == at, vec, 0.0), axis=1, keepdims=True)


def chol_solve_kernel(g_ref, p_ref, u_ref, x_ref, a_ref):
    n = g_ref.shape[0]
    m = p_ref.shape[0]
    width = BLOCK
    a_ref[...] = g_ref[...]
    u_ref[...] = jnp.zeros_like(u_ref)
    x_ref[...] = p_ref[...]
    full = lax.broadcasted_iota(jnp.int32, (1, n), 1)
    xwin = lax.broadcasted_iota(jnp.int32, (m, 128), 1)
    for lo in range(0, n, PHASE):
        c0 = (lo // 128) * 128
        nr = n - lo
        sub = lax.broadcasted_iota(jnp.int32, (nr, 1), 0) + lo
        lane = lax.broadcasted_iota(jnp.int32, (1, n - c0), 1) + c0
        win = lax.broadcasted_iota(jnp.int32, (nr, 128), 1)

        def step(t, carry, lo=lo, c0=c0, sub=sub, lane=lane, win=win):
            j0 = width * t
            base = pl.multiple_of((j0 // 128) * 128, 128)
            blk = a_ref[lo:, pl.ds(base, 128)]
            xblk = x_ref[:, pl.ds(base, 128)]
            raw = [a_ref[pl.ds(j0 + i, 1), :] for i in range(width)]
            entry = {(i, k): pick(raw[i], full, j0 + k) for i in range(width) for k in range(i, width)}
            low, inv = {}, []
            for i in range(width):
                d = entry[(i, i)]
                for q in range(i):
                    d = d - low[(i, q)] * low[(i, q)]
                inv.append(lax.rsqrt(d))
                for k in range(i + 1, width):
                    v = entry[(i, k)]
                    for q in range(i):
                        v = v - low[(k, q)] * low[(i, q)]
                    low[(k, i)] = v * inv[i]
            rows, cols, xs = [], [], []
            for i in range(width):
                j = j0 + i
                row = raw[i]
                col = pick(blk, win, j - base)
                xv = pick(xblk, xwin, j - base)
                for q in range(i):
                    row = row - low[(i, q)] * rows[q]
                    col = col - cols[q] * low[(i, q)]
                    xv = xv - xs[q] * low[(i, q)]
                rows.append(jnp.where(full >= j, row * inv[i], 0.0))
                cols.append(jnp.where(sub >= j, col * inv[i], 0.0))
                xs.append(xv * inv[i])
            update = cols[0] * rows[0][:, c0:]
            for i in range(1, width):
                update = update + cols[i] * rows[i][:, c0:]
            a_ref[lo:, c0:] = a_ref[lo:, c0:] - update
            for i in range(width):
                u_ref[pl.ds(j0 + i, 1), :] = rows[i]
            later = lane >= j0 + width
            rest = x_ref[:, c0:]
            for i in range(width):
                rest = rest - xs[i] * jnp.where(later, rows[i][:, c0:], 0.0)
            for i in range(width):
                rest = jnp.where(lane == j0 + i, xs[i], rest)
            x_ref[:, c0:] = rest
            return carry

        lax.fori_loop(lo // width, (lo + PHASE) // width, step, 0)


def chol_solve(g, p):
    n = g.shape[0]
    r = lax.broadcasted_iota(jnp.int32, (n, n), 0)
    c = lax.broadcasted_iota(jnp.int32, (n, n), 1)
    g = jnp.where(r >= c, g, g.T)
    return pl.pallas_call(
        chol_solve_kernel,
        out_shape=(jax.ShapeDtypeStruct((n, n), jnp.float32), jax.ShapeDtypeStruct(p.shape, jnp.float32)),
        in_specs=[pl.BlockSpec(memory_space=pltpu.VMEM)] * 2,
        out_specs=(pl.BlockSpec(memory_space=pltpu.VMEM), pl.BlockSpec(memory_space=pltpu.VMEM)),
        scratch_shapes=[pltpu.VMEM((n, n), jnp.float32)],
    )(g, p)


def group_size(axes):
    size = 1
    for axis in axes:
        size *= lax.axis_size(axis)
    return size


def exchange_sum(x, axes):
    size = group_size(axes)
    chunks = lax.all_to_all(x.reshape(size, -1, x.shape[-1]), axes, 0, 0, tiled=False)
    return jnp.sum(chunks, axis=0)


def exchange_gather(x, axes):
    size = group_size(axes)
    copies = jnp.broadcast_to(x[None], (size,) + x.shape)
    return lax.all_to_all(copies, axes, 0, 0, tiled=False).reshape(-1, x.shape[-1])


def pair_gather(x):
    other = lax.ppermute(x, "core", [(0, 1), (1, 0)])
    first = lax.axis_index("core") == 0
    low = jnp.where(first, x, other).reshape(lax.axis_size("chip"), -1, x.shape[-1])
    high = jnp.where(first, other, x).reshape(lax.axis_size("chip"), -1, x.shape[-1])
    return jnp.stack([low, high], axis=1).reshape(-1, x.shape[-1])


def pair_scatter_sum(x):
    chips = lax.axis_size("chip")
    pairs = x.reshape(chips, 2, -1, x.shape[-1])
    first = lax.axis_index("core") == 0
    keep = jnp.where(first, pairs[:, 0], pairs[:, 1])
    send = jnp.where(first, pairs[:, 1], pairs[:, 0])
    return (keep + lax.ppermute(send, "core", [(0, 1), (1, 0)])).reshape(-1, x.shape[-1])


def body(start_block, tile_values, tile_rows, tile_cols, tile_count):
    tile_size = tile_values.shape[-1]
    basis_width = start_block.shape[1]
    slot_total = tile_values.shape[2]
    slab = pair_gather(exchange_gather(start_block, ("chip",)))
    start_blocks = slab.reshape(-1, tile_size, basis_width)
    block_cols = start_blocks.shape[0]
    values = tile_values.reshape(slot_total, tile_size, tile_size)
    row_ids = tile_rows.reshape(slot_total)
    col_ids = tile_cols.reshape(slot_total)
    live_count = tile_count.reshape(())
    block_rows = BR
    live = jnp.arange(slot_total, dtype=jnp.int32) < live_count
    row_hit = (row_ids[:, None] == jnp.arange(block_rows, dtype=jnp.int32)[None, :]) & live[:, None]
    products = jnp.einsum(
        "tij,tjk->tik",
        values,
        start_blocks[col_ids],
        precision=lax.Precision.HIGHEST,
        preferred_element_type=jnp.float32,
    )
    partial_image = jnp.sum(
        jnp.where(row_hit[:, :, None, None], products[:, None], 0.0), axis=0
    )
    partial_rows = partial_image.reshape(-1, basis_width)
    image_block = exchange_gather(exchange_sum(partial_rows, ("col",)), ("col",))
    image_blocks = image_block.reshape(block_rows, tile_size, basis_width)
    col_hit = (col_ids[:, None] == jnp.arange(block_cols, dtype=jnp.int32)[None, :]) & live[:, None]
    back_products = jnp.einsum(
        "tji,tjk->tik",
        values,
        image_blocks[row_ids],
        precision=lax.Precision.HIGHEST,
        preferred_element_type=jnp.float32,
    )
    partial_projected = jnp.sum(
        jnp.where(col_hit[:, :, None, None], back_products[:, None], 0.0), axis=0
    )
    partial_flat = partial_projected.reshape(-1, basis_width)
    projected = exchange_sum(pair_scatter_sum(partial_flat), ("chip",))
    share_rows = projected.shape[0]
    matrix_order = share_rows * group_size(("chip", "core", "col"))
    local_gram = jnp.dot(
        projected.T, projected, precision=lax.Precision.HIGHEST, preferred_element_type=jnp.float32
    )
    spread = ("chip", "col")
    gram_rows = exchange_gather(exchange_sum(pair_scatter_sum(local_gram), spread), spread)
    gram_matrix = pair_gather(gram_rows) / matrix_order
    factor, new_basis = chol_solve(gram_matrix, projected)
    return (image_block, new_basis, factor)


def solution(mesh):
    devices = mesh.devices
    split = jax.sharding.Mesh(
        devices.reshape(devices.shape[0] // 2, 2, devices.shape[1]), ("chip", "core", "col")
    )
    rows = ("chip", "core")
    placed = (
        P(("col",) + rows, None),
        P(rows, "col", None, None, None),
        P(rows, "col", None),
        P(rows, "col", None),
        P(rows, "col"),
    )
    return jax.shard_map(
        body,
        mesh=split,
        in_specs=placed,
        out_specs=(P(rows, None), P(("col",) + rows, None), P()),
        check_vma=False,
    )
```

```python
import jax
import jax.numpy as jnp
from jax import lax
from jax.experimental import pallas as pl
from jax.experimental.pallas import tpu as pltpu
from jax.sharding import PartitionSpec as P

BR = 1


PHASE = 16
BLOCK = 4


def pick(vec, lanes, at):
    return jnp.sum(jnp.where(lanes == at, vec, 0.0), axis=1, keepdims=True)


def chol_solve_kernel(g_ref, p_ref, u_ref, x_ref, a_ref):
    n = g_ref.shape[0]
    m = p_ref.shape[0]
    width = BLOCK
    a_ref[...] = g_ref[...]
    u_ref[...] = jnp.zeros_like(u_ref)
    x_ref[...] = p_ref[...]
    full = lax.broadcasted_iota(jnp.int32, (1, n), 1)
    xwin = lax.broadcasted_iota(jnp.int32, (m, 128), 1)
    for lo in range(0, n, PHASE):
        c0 = (lo // 128) * 128
        nr = n - lo
        sub = lax.broadcasted_iota(jnp.int32, (nr, 1), 0) + lo
        lane = lax.broadcasted_iota(jnp.int32, (1, n - c0), 1) + c0
        win = lax.broadcasted_iota(jnp.int32, (nr, 128), 1)

        def step(t, carry, lo=lo, c0=c0, sub=sub, lane=lane, win=win):
            j0 = width * t
            base = pl.multiple_of((j0 // 128) * 128, 128)
            blk = a_ref[lo:, pl.ds(base, 128)]
            xblk = x_ref[:, pl.ds(base, 128)]
            raw = [a_ref[pl.ds(j0 + i, 1), :] for i in range(width)]
            entry = {(i, k): pick(raw[i], full, j0 + k) for i in range(width) for k in range(i, width)}
            low, inv = {}, []
            for i in range(width):
                d = entry[(i, i)]
                for q in range(i):
                    d = d - low[(i, q)] * low[(i, q)]
                inv.append(lax.rsqrt(d))
                for k in range(i + 1, width):
                    v = entry[(i, k)]
                    for q in range(i):
                        v = v - low[(k, q)] * low[(i, q)]
                    low[(k, i)] = v * inv[i]
            rows, cols, xs = [], [], []
            for i in range(width):
                j = j0 + i
                row = raw[i]
                col = pick(blk, win, j - base)
                xv = pick(xblk, xwin, j - base)
                for q in range(i):
                    row = row - low[(i, q)] * rows[q]
                    col = col - cols[q] * low[(i, q)]
                    xv = xv - xs[q] * low[(i, q)]
                rows.append(jnp.where(full >= j, row * inv[i], 0.0))
                cols.append(jnp.where(sub >= j, col * inv[i], 0.0))
                xs.append(xv * inv[i])
            update = cols[0] * rows[0][:, c0:]
            for i in range(1, width):
                update = update + cols[i] * rows[i][:, c0:]
            a_ref[lo:, c0:] = a_ref[lo:, c0:] - update
            for i in range(width):
                u_ref[pl.ds(j0 + i, 1), :] = rows[i]
            later = lane >= j0 + width
            rest = x_ref[:, c0:]
            for i in range(width):
                rest = rest - xs[i] * jnp.where(later, rows[i][:, c0:], 0.0)
            for i in range(width):
                rest = jnp.where(lane == j0 + i, xs[i], rest)
            x_ref[:, c0:] = rest
            return carry

        lax.fori_loop(lo // width, (lo + PHASE) // width, step, 0)


def chol_solve(g, p):
    n = g.shape[0]
    r = lax.broadcasted_iota(jnp.int32, (n, n), 0)
    c = lax.broadcasted_iota(jnp.int32, (n, n), 1)
    g = jnp.where(r >= c, g, g.T)
    return pl.pallas_call(
        chol_solve_kernel,
        out_shape=(jax.ShapeDtypeStruct((n, n), jnp.float32), jax.ShapeDtypeStruct(p.shape, jnp.float32)),
        in_specs=[pl.BlockSpec(memory_space=pltpu.VMEM)] * 2,
        out_specs=(pl.BlockSpec(memory_space=pltpu.VMEM), pl.BlockSpec(memory_space=pltpu.VMEM)),
        scratch_shapes=[pltpu.VMEM((n, n), jnp.float32)],
    )(g, p)


def group_size(axes):
    size = 1
    for axis in axes:
        size *= lax.axis_size(axis)
    return size


def exchange_sum(x, axes):
    size = group_size(axes)
    chunks = lax.all_to_all(x.reshape(size, -1, x.shape[-1]), axes, 0, 0, tiled=False)
    return jnp.sum(chunks, axis=0)


def exchange_gather(x, axes):
    size = group_size(axes)
    copies = jnp.broadcast_to(x[None], (size,) + x.shape)
    return lax.all_to_all(copies, axes, 0, 0, tiled=False).reshape(-1, x.shape[-1])


def pair_gather(x):
    other = lax.ppermute(x, "core", [(0, 1), (1, 0)])
    first = lax.axis_index("core") == 0
    low = jnp.where(first, x, other).reshape(lax.axis_size("chip"), -1, x.shape[-1])
    high = jnp.where(first, other, x).reshape(lax.axis_size("chip"), -1, x.shape[-1])
    return jnp.stack([low, high], axis=1).reshape(-1, x.shape[-1])


def pair_scatter_sum(x):
    chips = lax.axis_size("chip")
    pairs = x.reshape(chips, 2, -1, x.shape[-1])
    first = lax.axis_index("core") == 0
    keep = jnp.where(first, pairs[:, 0], pairs[:, 1])
    send = jnp.where(first, pairs[:, 1], pairs[:, 0])
    return (keep + lax.ppermute(send, "core", [(0, 1), (1, 0)])).reshape(-1, x.shape[-1])


def body(start_block, tile_values, tile_rows, tile_cols, tile_count):
    tile_size = tile_values.shape[-1]
    basis_width = start_block.shape[1]
    slot_total = tile_values.shape[2]
    slab = pair_gather(exchange_gather(start_block, ("chip",)))
    start_blocks = slab.reshape(-1, tile_size, basis_width)
    block_cols = start_blocks.shape[0]
    values = tile_values.reshape(slot_total, tile_size, tile_size)
    row_ids = tile_rows.reshape(slot_total)
    col_ids = tile_cols.reshape(slot_total)
    live_count = tile_count.reshape(())
    block_rows = BR
    live = jnp.arange(slot_total, dtype=jnp.int32) < live_count
    row_hit = (row_ids[:, None] == jnp.arange(block_rows, dtype=jnp.int32)[None, :]) & live[:, None]
    products = jnp.einsum(
        "tij,tjk->tik",
        values,
        start_blocks[col_ids],
        precision=lax.Precision.HIGHEST,
        preferred_element_type=jnp.float32,
    )
    partial_image = jnp.sum(
        jnp.where(row_hit[:, :, None, None], products[:, None], 0.0), axis=0
    )
    partial_rows = partial_image.reshape(-1, basis_width)
    image_block = exchange_gather(exchange_sum(partial_rows, ("col",)), ("col",))
    image_blocks = image_block.reshape(block_rows, tile_size, basis_width)
    col_hit = (col_ids[:, None] == jnp.arange(block_cols, dtype=jnp.int32)[None, :]) & live[:, None]
    back_products = jnp.einsum(
        "tji,tjk->tik",
        values,
        image_blocks[row_ids],
        precision=lax.Precision.HIGHEST,
        preferred_element_type=jnp.float32,
    )
    partial_projected = jnp.sum(
        jnp.where(col_hit[:, :, None, None], back_products[:, None], 0.0), axis=0
    )
    partial_flat = partial_projected.reshape(-1, basis_width)
    projected = exchange_sum(pair_scatter_sum(partial_flat), ("chip",))
    share_rows = projected.shape[0]
    matrix_order = share_rows * group_size(("chip", "core", "col"))
    local_gram = jnp.dot(
        projected.T, projected, precision=lax.Precision.HIGHEST, preferred_element_type=jnp.float32
    )
    spread = ("chip", "col")
    gram_rows = exchange_gather(exchange_sum(pair_scatter_sum(local_gram), spread), spread)
    gram_matrix = pair_gather(gram_rows) / matrix_order
    factor, new_basis = chol_solve(gram_matrix, projected)
    return (image_block, new_basis, factor)


def solution(mesh):
    devices = mesh.devices
    split = jax.sharding.Mesh(
        devices.reshape(devices.shape[0] // 2, 2, devices.shape[1]), ("chip", "core", "col")
    )
    rows = ("chip", "core")
    placed = (
        P(("col",) + rows, None),
        P(rows, "col", None, None, None),
        P(rows, "col", None),
        P(rows, "col", None),
        P(rows, "col"),
    )
    return jax.shard_map(
        body,
        mesh=split,
        in_specs=placed,
        out_specs=(P(rows, None), P(("col",) + rows, None), P()),
        check_vma=False,
    )
```

```python
import jax
import jax.numpy as jnp
from jax import lax
from jax.experimental import pallas as pl
from jax.experimental.pallas import tpu as pltpu
from jax.sharding import PartitionSpec as P

BR = 1


PHASE = 16
BLOCK = 4


def pick(vec, lanes, at):
    return jnp.sum(jnp.where(lanes == at, vec, 0.0), axis=1, keepdims=True)


def chol_solve_kernel(g_ref, p_ref, u_ref, x_ref, a_ref):
    n = g_ref.shape[0]
    m = p_ref.shape[0]
    width = BLOCK
    a_ref[...] = g_ref[...]
    u_ref[...] = jnp.zeros_like(u_ref)
    x_ref[...] = p_ref[...]
    full = lax.broadcasted_iota(jnp.int32, (1, n), 1)
    xwin = lax.broadcasted_iota(jnp.int32, (m, 128), 1)
    for lo in range(0, n, PHASE):
        c0 = (lo // 128) * 128
        nr = n - lo
        sub = lax.broadcasted_iota(jnp.int32, (nr, 1), 0) + lo
        lane = lax.broadcasted_iota(jnp.int32, (1, n - c0), 1) + c0
        win = lax.broadcasted_iota(jnp.int32, (nr, 128), 1)

        def step(t, carry, lo=lo, c0=c0, sub=sub, lane=lane, win=win):
            j0 = width * t
            base = pl.multiple_of((j0 // 128) * 128, 128)
            blk = a_ref[lo:, pl.ds(base, 128)]
            xblk = x_ref[:, pl.ds(base, 128)]
            raw = [a_ref[pl.ds(j0 + i, 1), :] for i in range(width)]
            entry = {(i, k): pick(raw[i], full, j0 + k) for i in range(width) for k in range(i, width)}
            low, inv = {}, []
            for i in range(width):
                d = entry[(i, i)]
                for q in range(i):
                    d = d - low[(i, q)] * low[(i, q)]
                inv.append(lax.rsqrt(d))
                for k in range(i + 1, width):
                    v = entry[(i, k)]
                    for q in range(i):
                        v = v - low[(k, q)] * low[(i, q)]
                    low[(k, i)] = v * inv[i]
            rows, cols, xs = [], [], []
            for i in range(width):
                j = j0 + i
                row = raw[i]
                col = pick(blk, win, j - base)
                xv = pick(xblk, xwin, j - base)
                for q in range(i):
                    row = row - low[(i, q)] * rows[q]
                    col = col - cols[q] * low[(i, q)]
                    xv = xv - xs[q] * low[(i, q)]
                rows.append(jnp.where(full >= j, row * inv[i], 0.0))
                cols.append(jnp.where(sub >= j, col * inv[i], 0.0))
                xs.append(xv * inv[i])
            update = cols[0] * rows[0][:, c0:]
            for i in range(1, width):
                update = update + cols[i] * rows[i][:, c0:]
            a_ref[lo:, c0:] = a_ref[lo:, c0:] - update
            for i in range(width):
                u_ref[pl.ds(j0 + i, 1), :] = rows[i]
            later = lane >= j0 + width
            rest = x_ref[:, c0:]
            for i in range(width):
                rest = rest - xs[i] * jnp.where(later, rows[i][:, c0:], 0.0)
            for i in range(width):
                rest = jnp.where(lane == j0 + i, xs[i], rest)
            x_ref[:, c0:] = rest
            return carry

        lax.fori_loop(lo // width, (lo + PHASE) // width, step, 0)


def chol_solve(g, p):
    n = g.shape[0]
    r = lax.broadcasted_iota(jnp.int32, (n, n), 0)
    c = lax.broadcasted_iota(jnp.int32, (n, n), 1)
    g = jnp.where(r >= c, g, g.T)
    return pl.pallas_call(
        chol_solve_kernel,
        out_shape=(jax.ShapeDtypeStruct((n, n), jnp.float32), jax.ShapeDtypeStruct(p.shape, jnp.float32)),
        in_specs=[pl.BlockSpec(memory_space=pltpu.VMEM)] * 2,
        out_specs=(pl.BlockSpec(memory_space=pltpu.VMEM), pl.BlockSpec(memory_space=pltpu.VMEM)),
        scratch_shapes=[pltpu.VMEM((n, n), jnp.float32)],
    )(g, p)


def group_size(axes):
    size = 1
    for axis in axes:
        size *= lax.axis_size(axis)
    return size


def exchange_sum(x, axes):
    size = group_size(axes)
    chunks = lax.all_to_all(x.reshape(size, -1, x.shape[-1]), axes, 0, 0, tiled=False)
    return jnp.sum(chunks, axis=0)


def exchange_gather(x, axes):
    size = group_size(axes)
    copies = jnp.broadcast_to(x[None], (size,) + x.shape)
    return lax.all_to_all(copies, axes, 0, 0, tiled=False).reshape(-1, x.shape[-1])


def pair_gather(x):
    other = lax.ppermute(x, "core", [(0, 1), (1, 0)])
    first = lax.axis_index("core") == 0
    low = jnp.where(first, x, other).reshape(lax.axis_size("chip"), -1, x.shape[-1])
    high = jnp.where(first, other, x).reshape(lax.axis_size("chip"), -1, x.shape[-1])
    return jnp.stack([low, high], axis=1).reshape(-1, x.shape[-1])


def pair_scatter_sum(x):
    chips = lax.axis_size("chip")
    pairs = x.reshape(chips, 2, -1, x.shape[-1])
    first = lax.axis_index("core") == 0
    keep = jnp.where(first, pairs[:, 0], pairs[:, 1])
    send = jnp.where(first, pairs[:, 1], pairs[:, 0])
    return (keep + lax.ppermute(send, "core", [(0, 1), (1, 0)])).reshape(-1, x.shape[-1])


def body(start_block, tile_values, tile_rows, tile_cols, tile_count):
    tile_size = tile_values.shape[-1]
    basis_width = start_block.shape[1]
    slot_total = tile_values.shape[2]
    slab = pair_gather(exchange_gather(start_block, ("chip",)))
    start_blocks = slab.reshape(-1, tile_size, basis_width)
    block_cols = start_blocks.shape[0]
    values = tile_values.reshape(slot_total, tile_size, tile_size)
    row_ids = tile_rows.reshape(slot_total)
    col_ids = tile_cols.reshape(slot_total)
    live_count = tile_count.reshape(())
    block_rows = BR
    live = jnp.arange(slot_total, dtype=jnp.int32) < live_count
    row_hit = (row_ids[:, None] == jnp.arange(block_rows, dtype=jnp.int32)[None, :]) & live[:, None]
    products = jnp.stack(
        [
            jnp.dot(
                values[slot],
                lax.dynamic_index_in_dim(start_blocks, col_ids[slot], 0, keepdims=False),
                precision=lax.Precision.HIGHEST,
                preferred_element_type=jnp.float32,
            )
            for slot in range(slot_total)
        ]
    )
    partial_image = jnp.sum(
        jnp.where(row_hit[:, :, None, None], products[:, None], 0.0), axis=0
    )
    partial_rows = partial_image.reshape(-1, basis_width)
    image_block = exchange_gather(exchange_sum(partial_rows, ("col",)), ("col",))
    image_blocks = image_block.reshape(block_rows, tile_size, basis_width)
    col_hit = (col_ids[:, None] == jnp.arange(block_cols, dtype=jnp.int32)[None, :]) & live[:, None]
    back_products = jnp.einsum(
        "tji,tjk->tik",
        values,
        image_blocks[row_ids],
        precision=lax.Precision.HIGHEST,
        preferred_element_type=jnp.float32,
    )
    partial_projected = jnp.sum(
        jnp.where(col_hit[:, :, None, None], back_products[:, None], 0.0), axis=0
    )
    partial_flat = partial_projected.reshape(-1, basis_width)
    projected = exchange_sum(pair_scatter_sum(partial_flat), ("chip",))
    share_rows = projected.shape[0]
    matrix_order = share_rows * group_size(("chip", "core", "col"))
    local_gram = jnp.dot(
        projected.T, projected, precision=lax.Precision.HIGHEST, preferred_element_type=jnp.float32
    )
    spread = ("chip", "col")
    gram_rows = exchange_gather(exchange_sum(pair_scatter_sum(local_gram), spread), spread)
    gram_matrix = pair_gather(gram_rows) / matrix_order
    factor, new_basis = chol_solve(gram_matrix, projected)
    return (image_block, new_basis, factor)


def solution(mesh):
    devices = mesh.devices
    split = jax.sharding.Mesh(
        devices.reshape(devices.shape[0] // 2, 2, devices.shape[1]), ("chip", "core", "col")
    )
    rows = ("chip", "core")
    placed = (
        P(("col",) + rows, None),
        P(rows, "col", None, None, None),
        P(rows, "col", None),
        P(rows, "col", None),
        P(rows, "col"),
    )
    return jax.shard_map(
        body,
        mesh=split,
        in_specs=placed,
        out_specs=(P(rows, None), P(("col",) + rows, None), P()),
        check_vma=False,
    )
```

```python
import jax
import jax.numpy as jnp
from jax import lax
from jax.experimental import pallas as pl
from jax.experimental.pallas import tpu as pltpu
from jax.sharding import PartitionSpec as P

BR = 1


PHASE = 16
BLOCK = 4


def pick(vec, lanes, at):
    return jnp.sum(jnp.where(lanes == at, vec, 0.0), axis=1, keepdims=True)


def chol_solve_kernel(g_ref, p_ref, u_ref, x_ref, a_ref):
    n = g_ref.shape[0]
    m = p_ref.shape[0]
    width = BLOCK
    a_ref[...] = g_ref[...]
    u_ref[...] = jnp.zeros_like(u_ref)
    x_ref[...] = p_ref[...]
    full = lax.broadcasted_iota(jnp.int32, (1, n), 1)
    xwin = lax.broadcasted_iota(jnp.int32, (m, 128), 1)
    for lo in range(0, n, PHASE):
        c0 = (lo // 128) * 128
        nr = n - lo
        sub = lax.broadcasted_iota(jnp.int32, (nr, 1), 0) + lo
        lane = lax.broadcasted_iota(jnp.int32, (1, n - c0), 1) + c0
        win = lax.broadcasted_iota(jnp.int32, (nr, 128), 1)

        def step(t, carry, lo=lo, c0=c0, sub=sub, lane=lane, win=win):
            j0 = width * t
            base = pl.multiple_of((j0 // 128) * 128, 128)
            blk = a_ref[lo:, pl.ds(base, 128)]
            xblk = x_ref[:, pl.ds(base, 128)]
            raw = [a_ref[pl.ds(j0 + i, 1), :] for i in range(width)]
            entry = {(i, k): pick(raw[i], full, j0 + k) for i in range(width) for k in range(i, width)}
            low, inv = {}, []
            for i in range(width):
                d = entry[(i, i)]
                for q in range(i):
                    d = d - low[(i, q)] * low[(i, q)]
                inv.append(lax.rsqrt(d))
                for k in range(i + 1, width):
                    v = entry[(i, k)]
                    for q in range(i):
                        v = v - low[(k, q)] * low[(i, q)]
                    low[(k, i)] = v * inv[i]
            rows, cols, xs = [], [], []
            for i in range(width):
                j = j0 + i
                row = raw[i]
                col = pick(blk, win, j - base)
                xv = pick(xblk, xwin, j - base)
                for q in range(i):
                    row = row - low[(i, q)] * rows[q]
                    col = col - cols[q] * low[(i, q)]
                    xv = xv - xs[q] * low[(i, q)]
                rows.append(jnp.where(full >= j, row * inv[i], 0.0))
                cols.append(jnp.where(sub >= j, col * inv[i], 0.0))
                xs.append(xv * inv[i])
            update = cols[0] * rows[0][:, c0:]
            for i in range(1, width):
                update = update + cols[i] * rows[i][:, c0:]
            a_ref[lo:, c0:] = a_ref[lo:, c0:] - update
            for i in range(width):
                u_ref[pl.ds(j0 + i, 1), :] = rows[i]
            later = lane >= j0 + width
            rest = x_ref[:, c0:]
            for i in range(width):
                rest = rest - xs[i] * jnp.where(later, rows[i][:, c0:], 0.0)
            for i in range(width):
                rest = jnp.where(lane == j0 + i, xs[i], rest)
            x_ref[:, c0:] = rest
            return carry

        lax.fori_loop(lo // width, (lo + PHASE) // width, step, 0)


def chol_solve(g, p):
    n = g.shape[0]
    r = lax.broadcasted_iota(jnp.int32, (n, n), 0)
    c = lax.broadcasted_iota(jnp.int32, (n, n), 1)
    g = jnp.where(r >= c, g, g.T)
    return pl.pallas_call(
        chol_solve_kernel,
        out_shape=(jax.ShapeDtypeStruct((n, n), jnp.float32), jax.ShapeDtypeStruct(p.shape, jnp.float32)),
        in_specs=[pl.BlockSpec(memory_space=pltpu.VMEM)] * 2,
        out_specs=(pl.BlockSpec(memory_space=pltpu.VMEM), pl.BlockSpec(memory_space=pltpu.VMEM)),
        scratch_shapes=[pltpu.VMEM((n, n), jnp.float32)],
    )(g, p)


def group_size(axes):
    size = 1
    for axis in axes:
        size *= lax.axis_size(axis)
    return size


def exchange_sum(x, axes):
    size = group_size(axes)
    chunks = lax.all_to_all(x.reshape(size, -1, x.shape[-1]), axes, 0, 0, tiled=False)
    return jnp.sum(chunks, axis=0)


def exchange_gather(x, axes):
    size = group_size(axes)
    copies = jnp.broadcast_to(x[None], (size,) + x.shape)
    return lax.all_to_all(copies, axes, 0, 0, tiled=False).reshape(-1, x.shape[-1])


def pair_gather(x):
    other = lax.ppermute(x, "core", [(0, 1), (1, 0)])
    first = lax.axis_index("core") == 0
    low = jnp.where(first, x, other).reshape(lax.axis_size("chip"), -1, x.shape[-1])
    high = jnp.where(first, other, x).reshape(lax.axis_size("chip"), -1, x.shape[-1])
    return jnp.stack([low, high], axis=1).reshape(-1, x.shape[-1])


def pair_scatter_sum(x):
    chips = lax.axis_size("chip")
    pairs = x.reshape(chips, 2, -1, x.shape[-1])
    core = lax.axis_index("core")
    keep = lax.dynamic_index_in_dim(pairs, core, 1, keepdims=False)
    send = lax.dynamic_index_in_dim(pairs, 1 - core, 1, keepdims=False)
    return (keep + lax.ppermute(send, "core", [(0, 1), (1, 0)])).reshape(-1, x.shape[-1])


def body(start_block, tile_values, tile_rows, tile_cols, tile_count):
    tile_size = tile_values.shape[-1]
    basis_width = start_block.shape[1]
    slot_total = tile_values.shape[2]
    slab = pair_gather(exchange_gather(start_block, ("chip",)))
    start_blocks = slab.reshape(-1, tile_size, basis_width)
    block_cols = start_blocks.shape[0]
    values = tile_values.reshape(slot_total, tile_size, tile_size)
    row_ids = tile_rows.reshape(slot_total)
    col_ids = tile_cols.reshape(slot_total)
    live_count = tile_count.reshape(())
    block_rows = BR
    live = jnp.arange(slot_total, dtype=jnp.int32) < live_count
    row_hit = (row_ids[:, None] == jnp.arange(block_rows, dtype=jnp.int32)[None, :]) & live[:, None]
    products = jnp.einsum(
        "tij,tjk->tik",
        values,
        start_blocks[col_ids],
        precision=lax.Precision.HIGHEST,
        preferred_element_type=jnp.float32,
    )
    partial_image = jnp.sum(
        jnp.where(row_hit[:, :, None, None], products[:, None], 0.0), axis=0
    )
    partial_rows = partial_image.reshape(-1, basis_width)
    image_block = exchange_gather(exchange_sum(partial_rows, ("col",)), ("col",))
    image_blocks = image_block.reshape(block_rows, tile_size, basis_width)
    col_hit = (col_ids[:, None] == jnp.arange(block_cols, dtype=jnp.int32)[None, :]) & live[:, None]
    back_products = jnp.einsum(
        "tji,tjk->tik",
        values,
        image_blocks[row_ids],
        precision=lax.Precision.HIGHEST,
        preferred_element_type=jnp.float32,
    )
    partial_projected = jnp.sum(
        jnp.where(col_hit[:, :, None, None], back_products[:, None], 0.0), axis=0
    )
    partial_flat = partial_projected.reshape(-1, basis_width)
    projected = exchange_sum(pair_scatter_sum(partial_flat), ("chip",))
    share_rows = projected.shape[0]
    matrix_order = share_rows * group_size(("chip", "core", "col"))
    local_gram = jnp.dot(
        projected.T, projected, precision=lax.Precision.HIGHEST, preferred_element_type=jnp.float32
    )
    spread = ("chip", "col")
    gram_rows = exchange_gather(exchange_sum(pair_scatter_sum(local_gram), spread), spread)
    gram_matrix = pair_gather(gram_rows) / matrix_order
    factor, new_basis = chol_solve(gram_matrix, projected)
    return (image_block, new_basis, factor)


def solution(mesh):
    devices = mesh.devices
    split = jax.sharding.Mesh(
        devices.reshape(devices.shape[0] // 2, 2, devices.shape[1]), ("chip", "core", "col")
    )
    rows = ("chip", "core")
    placed = (
        P(("col",) + rows, None),
        P(rows, "col", None, None, None),
        P(rows, "col", None),
        P(rows, "col", None),
        P(rows, "col"),
    )
    return jax.shard_map(
        body,
        mesh=split,
        in_specs=placed,
        out_specs=(P(rows, None), P(("col",) + rows, None), P()),
        check_vma=False,
    )
```

```python
import jax
import jax.numpy as jnp
from jax import lax
from jax.experimental import pallas as pl
from jax.experimental.pallas import tpu as pltpu
from jax.sharding import PartitionSpec as P

BR = 1


PHASE = 16
BLOCK = 4


def pick(vec, lanes, at):
    return jnp.sum(jnp.where(lanes == at, vec, 0.0), axis=1, keepdims=True)


def chol_solve_kernel(g_ref, p_ref, u_ref, x_ref, a_ref):
    n = g_ref.shape[0]
    m = p_ref.shape[0]
    width = BLOCK
    a_ref[...] = g_ref[...]
    u_ref[...] = jnp.zeros_like(u_ref)
    x_ref[...] = p_ref[...]
    full = lax.broadcasted_iota(jnp.int32, (1, n), 1)
    xwin = lax.broadcasted_iota(jnp.int32, (m, 128), 1)
    for lo in range(0, n, PHASE):
        c0 = (lo // 128) * 128
        nr = n - lo
        sub = lax.broadcasted_iota(jnp.int32, (nr, 1), 0) + lo
        lane = lax.broadcasted_iota(jnp.int32, (1, n - c0), 1) + c0
        win = lax.broadcasted_iota(jnp.int32, (nr, 128), 1)

        def step(t, carry, lo=lo, c0=c0, sub=sub, lane=lane, win=win):
            j0 = width * t
            base = pl.multiple_of((j0 // 128) * 128, 128)
            blk = a_ref[lo:, pl.ds(base, 128)]
            xblk = x_ref[:, pl.ds(base, 128)]
            raw = [a_ref[pl.ds(j0 + i, 1), :] for i in range(width)]
            entry = {(i, k): pick(raw[i], full, j0 + k) for i in range(width) for k in range(i, width)}
            low, inv = {}, []
            for i in range(width):
                d = entry[(i, i)]
                for q in range(i):
                    d = d - low[(i, q)] * low[(i, q)]
                inv.append(lax.rsqrt(d))
                for k in range(i + 1, width):
                    v = entry[(i, k)]
                    for q in range(i):
                        v = v - low[(k, q)] * low[(i, q)]
                    low[(k, i)] = v * inv[i]
            rows, cols, xs = [], [], []
            for i in range(width):
                j = j0 + i
                row = raw[i]
                col = pick(blk, win, j - base)
                xv = pick(xblk, xwin, j - base)
                for q in range(i):
                    row = row - low[(i, q)] * rows[q]
                    col = col - cols[q] * low[(i, q)]
                    xv = xv - xs[q] * low[(i, q)]
                rows.append(jnp.where(full >= j, row * inv[i], 0.0))
                cols.append(jnp.where(sub >= j, col * inv[i], 0.0))
                xs.append(xv * inv[i])
            update = cols[0] * rows[0][:, c0:]
            for i in range(1, width):
                update = update + cols[i] * rows[i][:, c0:]
            a_ref[lo:, c0:] = a_ref[lo:, c0:] - update
            for i in range(width):
                u_ref[pl.ds(j0 + i, 1), :] = rows[i]
            later = lane >= j0 + width
            rest = x_ref[:, c0:]
            for i in range(width):
                rest = rest - xs[i] * jnp.where(later, rows[i][:, c0:], 0.0)
            for i in range(width):
                rest = jnp.where(lane == j0 + i, xs[i], rest)
            x_ref[:, c0:] = rest
            return carry

        lax.fori_loop(lo // width, (lo + PHASE) // width, step, 0)


def chol_solve(g, p):
    n = g.shape[0]
    r = lax.broadcasted_iota(jnp.int32, (n, n), 0)
    c = lax.broadcasted_iota(jnp.int32, (n, n), 1)
    g = jnp.where(r >= c, g, g.T)
    return pl.pallas_call(
        chol_solve_kernel,
        out_shape=(jax.ShapeDtypeStruct((n, n), jnp.float32), jax.ShapeDtypeStruct(p.shape, jnp.float32)),
        in_specs=[pl.BlockSpec(memory_space=pltpu.VMEM)] * 2,
        out_specs=(pl.BlockSpec(memory_space=pltpu.VMEM), pl.BlockSpec(memory_space=pltpu.VMEM)),
        scratch_shapes=[pltpu.VMEM((n, n), jnp.float32)],
    )(g, p)


def group_size(axes):
    size = 1
    for axis in axes:
        size *= lax.axis_size(axis)
    return size


def exchange_sum(x, axes):
    size = group_size(axes)
    chunks = lax.all_to_all(x.reshape(size, -1, x.shape[-1]), axes, 0, 0, tiled=False)
    return jnp.sum(chunks, axis=0)


def exchange_gather(x, axes):
    size = group_size(axes)
    copies = jnp.broadcast_to(x[None], (size,) + x.shape)
    return lax.all_to_all(copies, axes, 0, 0, tiled=False).reshape(-1, x.shape[-1])


def pair_gather(x):
    other = lax.ppermute(x, "core", [(0, 1), (1, 0)])
    core = lax.axis_index("core")
    both = jnp.stack([x, other]).reshape(2, lax.axis_size("chip"), -1, x.shape[-1])
    low = lax.dynamic_index_in_dim(both, core, 0, keepdims=False)
    high = lax.dynamic_index_in_dim(both, 1 - core, 0, keepdims=False)
    return jnp.stack([low, high], axis=1).reshape(-1, x.shape[-1])


def pair_scatter_sum(x):
    chips = lax.axis_size("chip")
    pairs = x.reshape(chips, 2, -1, x.shape[-1])
    core = lax.axis_index("core")
    keep = lax.dynamic_index_in_dim(pairs, core, 1, keepdims=False)
    send = lax.dynamic_index_in_dim(pairs, 1 - core, 1, keepdims=False)
    return (keep + lax.ppermute(send, "core", [(0, 1), (1, 0)])).reshape(-1, x.shape[-1])


def body(start_block, tile_values, tile_rows, tile_cols, tile_count):
    tile_size = tile_values.shape[-1]
    basis_width = start_block.shape[1]
    slot_total = tile_values.shape[2]
    slab = pair_gather(exchange_gather(start_block, ("chip",)))
    start_blocks = slab.reshape(-1, tile_size, basis_width)
    block_cols = start_blocks.shape[0]
    values = tile_values.reshape(slot_total, tile_size, tile_size)
    row_ids = tile_rows.reshape(slot_total)
    col_ids = tile_cols.reshape(slot_total)
    live_count = tile_count.reshape(())
    block_rows = BR
    live = jnp.arange(slot_total, dtype=jnp.int32) < live_count
    row_hit = (row_ids[:, None] == jnp.arange(block_rows, dtype=jnp.int32)[None, :]) & live[:, None]
    products = jnp.einsum(
        "tij,tjk->tik",
        values,
        start_blocks[col_ids],
        precision=lax.Precision.HIGHEST,
        preferred_element_type=jnp.float32,
    )
    partial_image = jnp.sum(
        jnp.where(row_hit[:, :, None, None], products[:, None], 0.0), axis=0
    )
    partial_rows = partial_image.reshape(-1, basis_width)
    image_block = exchange_gather(exchange_sum(partial_rows, ("col",)), ("col",))
    image_blocks = image_block.reshape(block_rows, tile_size, basis_width)
    col_hit = (col_ids[:, None] == jnp.arange(block_cols, dtype=jnp.int32)[None, :]) & live[:, None]
    back_products = jnp.einsum(
        "tji,tjk->tik",
        values,
        image_blocks[row_ids],
        precision=lax.Precision.HIGHEST,
        preferred_element_type=jnp.float32,
    )
    partial_projected = jnp.sum(
        jnp.where(col_hit[:, :, None, None], back_products[:, None], 0.0), axis=0
    )
    partial_flat = partial_projected.reshape(-1, basis_width)
    projected = exchange_sum(pair_scatter_sum(partial_flat), ("chip",))
    share_rows = projected.shape[0]
    matrix_order = share_rows * group_size(("chip", "core", "col"))
    local_gram = jnp.dot(
        projected.T, projected, precision=lax.Precision.HIGHEST, preferred_element_type=jnp.float32
    )
    spread = ("chip", "col")
    gram_rows = exchange_gather(exchange_sum(pair_scatter_sum(local_gram), spread), spread)
    gram_matrix = pair_gather(gram_rows) / matrix_order
    factor, new_basis = chol_solve(gram_matrix, projected)
    return (image_block, new_basis, factor)


def solution(mesh):
    devices = mesh.devices
    split = jax.sharding.Mesh(
        devices.reshape(devices.shape[0] // 2, 2, devices.shape[1]), ("chip", "core", "col")
    )
    rows = ("chip", "core")
    placed = (
        P(("col",) + rows, None),
        P(rows, "col", None, None, None),
        P(rows, "col", None),
        P(rows, "col", None),
        P(rows, "col"),
    )
    return jax.shard_map(
        body,
        mesh=split,
        in_specs=placed,
        out_specs=(P(rows, None), P(("col",) + rows, None), P()),
        check_vma=False,
    )
```

```python
import jax
import jax.numpy as jnp
from jax import lax
from jax.experimental import pallas as pl
from jax.experimental.pallas import tpu as pltpu
from jax.sharding import PartitionSpec as P

BR = 1


PHASE = 16
BLOCK = 4


def pick(vec, lanes, at):
    return jnp.sum(jnp.where(lanes == at, vec, 0.0), axis=1, keepdims=True)


def chol_solve_kernel(g_ref, p_ref, u_ref, x_ref, a_ref):
    n = g_ref.shape[0]
    m = p_ref.shape[0]
    width = BLOCK
    a_ref[...] = g_ref[...]
    x_ref[...] = p_ref[...]
    full = lax.broadcasted_iota(jnp.int32, (1, n), 1)
    xwin = lax.broadcasted_iota(jnp.int32, (m, 128), 1)
    for lo in range(0, n, PHASE):
        c0 = (lo // 128) * 128
        nr = n - lo
        sub = lax.broadcasted_iota(jnp.int32, (nr, 1), 0) + lo
        lane = lax.broadcasted_iota(jnp.int32, (1, n - c0), 1) + c0
        win = lax.broadcasted_iota(jnp.int32, (nr, 128), 1)

        def step(t, carry, lo=lo, c0=c0, sub=sub, lane=lane, win=win):
            j0 = width * t
            base = pl.multiple_of((j0 // 128) * 128, 128)
            blk = a_ref[lo:, pl.ds(base, 128)]
            xblk = x_ref[:, pl.ds(base, 128)]
            raw = [a_ref[pl.ds(j0 + i, 1), :] for i in range(width)]
            entry = {(i, k): pick(raw[i], full, j0 + k) for i in range(width) for k in range(i, width)}
            low, inv = {}, []
            for i in range(width):
                d = entry[(i, i)]
                for q in range(i):
                    d = d - low[(i, q)] * low[(i, q)]
                inv.append(lax.rsqrt(d))
                for k in range(i + 1, width):
                    v = entry[(i, k)]
                    for q in range(i):
                        v = v - low[(k, q)] * low[(i, q)]
                    low[(k, i)] = v * inv[i]
            rows, cols, xs = [], [], []
            for i in range(width):
                j = j0 + i
                row = raw[i]
                col = pick(blk, win, j - base)
                xv = pick(xblk, xwin, j - base)
                for q in range(i):
                    row = row - low[(i, q)] * rows[q]
                    col = col - cols[q] * low[(i, q)]
                    xv = xv - xs[q] * low[(i, q)]
                rows.append(jnp.where(full >= j, row * inv[i], 0.0))
                cols.append(jnp.where(sub >= j, col * inv[i], 0.0))
                xs.append(xv * inv[i])
            update = cols[0] * rows[0][:, c0:]
            for i in range(1, width):
                update = update + cols[i] * rows[i][:, c0:]
            a_ref[lo:, c0:] = a_ref[lo:, c0:] - update
            for i in range(width):
                u_ref[pl.ds(j0 + i, 1), :] = rows[i]
            later = lane >= j0 + width
            rest = x_ref[:, c0:]
            for i in range(width):
                rest = rest - xs[i] * jnp.where(later, rows[i][:, c0:], 0.0)
            for i in range(width):
                rest = jnp.where(lane == j0 + i, xs[i], rest)
            x_ref[:, c0:] = rest
            return carry

        lax.fori_loop(lo // width, (lo + PHASE) // width, step, 0)


def chol_solve(g, p):
    n = g.shape[0]
    r = lax.broadcasted_iota(jnp.int32, (n, n), 0)
    c = lax.broadcasted_iota(jnp.int32, (n, n), 1)
    g = jnp.where(r >= c, g, g.T)
    return pl.pallas_call(
        chol_solve_kernel,
        out_shape=(jax.ShapeDtypeStruct((n, n), jnp.float32), jax.ShapeDtypeStruct(p.shape, jnp.float32)),
        in_specs=[pl.BlockSpec(memory_space=pltpu.VMEM)] * 2,
        out_specs=(pl.BlockSpec(memory_space=pltpu.VMEM), pl.BlockSpec(memory_space=pltpu.VMEM)),
        scratch_shapes=[pltpu.VMEM((n, n), jnp.float32)],
    )(g, p)


def group_size(axes):
    size = 1
    for axis in axes:
        size *= lax.axis_size(axis)
    return size


def exchange_sum(x, axes):
    size = group_size(axes)
    chunks = lax.all_to_all(x.reshape(size, -1, x.shape[-1]), axes, 0, 0, tiled=False)
    return jnp.sum(chunks, axis=0)


def exchange_gather(x, axes):
    size = group_size(axes)
    copies = jnp.broadcast_to(x[None], (size,) + x.shape)
    return lax.all_to_all(copies, axes, 0, 0, tiled=False).reshape(-1, x.shape[-1])


def pair_gather(x):
    other = lax.ppermute(x, "core", [(0, 1), (1, 0)])
    core = lax.axis_index("core")
    both = jnp.stack([x, other]).reshape(2, lax.axis_size("chip"), -1, x.shape[-1])
    low = lax.dynamic_index_in_dim(both, core, 0, keepdims=False)
    high = lax.dynamic_index_in_dim(both, 1 - core, 0, keepdims=False)
    return jnp.stack([low, high], axis=1).reshape(-1, x.shape[-1])


def pair_scatter_sum(x):
    chips = lax.axis_size("chip")
    pairs = x.reshape(chips, 2, -1, x.shape[-1])
    core = lax.axis_index("core")
    keep = lax.dynamic_index_in_dim(pairs, core, 1, keepdims=False)
    send = lax.dynamic_index_in_dim(pairs, 1 - core, 1, keepdims=False)
    return (keep + lax.ppermute(send, "core", [(0, 1), (1, 0)])).reshape(-1, x.shape[-1])


def body(start_block, tile_values, tile_rows, tile_cols, tile_count):
    tile_size = tile_values.shape[-1]
    basis_width = start_block.shape[1]
    slot_total = tile_values.shape[2]
    slab = pair_gather(exchange_gather(start_block, ("chip",)))
    start_blocks = slab.reshape(-1, tile_size, basis_width)
    block_cols = start_blocks.shape[0]
    values = tile_values.reshape(slot_total, tile_size, tile_size)
    row_ids = tile_rows.reshape(slot_total)
    col_ids = tile_cols.reshape(slot_total)
    live_count = tile_count.reshape(())
    block_rows = BR
    live = jnp.arange(slot_total, dtype=jnp.int32) < live_count
    row_hit = (row_ids[:, None] == jnp.arange(block_rows, dtype=jnp.int32)[None, :]) & live[:, None]
    products = jnp.einsum(
        "tij,tjk->tik",
        values,
        start_blocks[col_ids],
        precision=lax.Precision.HIGHEST,
        preferred_element_type=jnp.float32,
    )
    partial_image = jnp.sum(
        jnp.where(row_hit[:, :, None, None], products[:, None], 0.0), axis=0
    )
    partial_rows = partial_image.reshape(-1, basis_width)
    image_block = exchange_gather(exchange_sum(partial_rows, ("col",)), ("col",))
    image_blocks = image_block.reshape(block_rows, tile_size, basis_width)
    col_hit = (col_ids[:, None] == jnp.arange(block_cols, dtype=jnp.int32)[None, :]) & live[:, None]
    back_products = jnp.einsum(
        "tji,tjk->tik",
        values,
        image_blocks[row_ids],
        precision=lax.Precision.HIGHEST,
        preferred_element_type=jnp.float32,
    )
    partial_projected = jnp.sum(
        jnp.where(col_hit[:, :, None, None], back_products[:, None], 0.0), axis=0
    )
    partial_flat = partial_projected.reshape(-1, basis_width)
    projected = exchange_sum(pair_scatter_sum(partial_flat), ("chip",))
    share_rows = projected.shape[0]
    matrix_order = share_rows * group_size(("chip", "core", "col"))
    local_gram = jnp.dot(
        projected.T, projected, precision=lax.Precision.HIGHEST, preferred_element_type=jnp.float32
    )
    spread = ("chip", "col")
    gram_rows = exchange_gather(exchange_sum(pair_scatter_sum(local_gram), spread), spread)
    gram_matrix = pair_gather(gram_rows) / matrix_order
    factor, new_basis = chol_solve(gram_matrix, projected)
    return (image_block, new_basis, factor)


def solution(mesh):
    devices = mesh.devices
    split = jax.sharding.Mesh(
        devices.reshape(devices.shape[0] // 2, 2, devices.shape[1]), ("chip", "core", "col")
    )
    rows = ("chip", "core")
    placed = (
        P(("col",) + rows, None),
        P(rows, "col", None, None, None),
        P(rows, "col", None),
        P(rows, "col", None),
        P(rows, "col"),
    )
    return jax.shard_map(
        body,
        mesh=split,
        in_specs=placed,
        out_specs=(P(rows, None), P(("col",) + rows, None), P()),
        check_vma=False,
    )
```
